256 devices in a mesh: lat: 8 (over x, y_hi), lon: 32 (over z, y_lo, core).
Axes of the slice: x: 4, y: 4 (y_hi: 2, y_lo: 2; y = y_hi * 2 + y_lo), z: 8, core: 2. Of those that a mesh axis runs over, the one named last changes fastest.
Arguments:
- probes: float32 [8, 4, 2048, 1024], P(None, None, 'lon', 'lat'), may hold values from -6 to 6
- wind: float32 [2, 4, 2048, 1024], P(None, None, 'lon', 'lat'), may hold values from -0.45 to 0.45
- wind_tend: float32 [2, 4, 2048, 1024], P(None, None, 'lon', 'lat'), may hold values from -0.05 to 0.05
- obs_weight: float32 [4, 2048, 1024], P(None, 'lon', 'lat'), may hold values from 0.5 to 18
Outputs:
- basis: float32 [8, 4, 2048, 1024], P(None, None, 'lon', 'lat')
- factor: float32 [8, 8], replicated
The draws below stay inside these ranges and needn't reach their ends.
All inputs are finite; a program needn't handle non-finite values.
Results may differ from the reference program's by a relative error of at most 0.00012.
Values sent between devices are 32-bit elements; how exact they have to be, the bound alone decides.
No kernel may reach another device: no remote copies, remote signals or barrier semaphores. Data moves between devices by JAX's collectives and lax.ppermute only.
A program may use at most 64 MiB of HBM per device.

```python
import math
import jax
import jax.numpy as jnp
from jax import lax

PROBES = 8
STEPS = 4
LEV = 4
NLON = 2048
NLAT = 1024
NCELLS = 8388608


def draw_obs_weight(key, part):
    noise = jax.random.uniform(key, (LEV, NLON, NLAT), jnp.float32)
    scale = jnp.exp(math.log(0.5) + noise * (math.log(2.0) - math.log(0.5)))
    lon_ramp = 1.0 + 2.0 * jnp.arange(NLON, dtype=jnp.float32) / NLON
    lat_ramp = 1.0 + 2.0 * jnp.arange(NLAT, dtype=jnp.float32) / NLAT
    return scale * lon_ramp[:, None] * lat_ramp[None, :]


def draw_wind(key, part):
    key_east = jax.random.fold_in(key, 11)
    key_north = jax.random.fold_in(key, 12)
    key_size = jax.random.fold_in(key, 13)
    lon_cells = jnp.arange(NLON, dtype=jnp.int32)
    lat_cells = jnp.arange(NLAT, dtype=jnp.int32)
    east_phase = jax.random.randint(key_east, (LEV, 1, NLAT), 0, 8)
    north_phase = jax.random.randint(key_north, (LEV, NLON, 1), 0, 8)
    east_sign = jnp.where((lon_cells[None, :, None] + east_phase) % 8 < 4, 1.0, -1.0)
    north_sign = jnp.where((lat_cells[None, None, :] + north_phase) % 8 < 4, 1.0, -1.0)
    signs = jnp.stack((east_sign, north_sign)).astype(jnp.float32)
    noise = jax.random.uniform(key_size, (2, LEV, NLON, NLAT), jnp.float32)
    size = 0.25 + 0.2 * noise
    return signs * size


def level_of(key, dims, cuts, smallest, high):
    factor_of, own = 1.0, jax.random.fold_in(key, 6)
    for dim, blocks in cuts:
        heights = jnp.exp(jax.random.uniform(jax.random.fold_in(own, dim), (blocks,), jnp.float32, smallest / len(cuts), high / len(cuts)))
        factor_of = factor_of * jnp.repeat(heights, dims[dim] // blocks).reshape([-1 if axis == dim else 1 for axis in range(len(dims))])
    return factor_of


def normal_values(stream_key, shape, scale, most, pieces=(), kind=jnp.bfloat16):
    array = jax.random.normal(stream_key, shape, jnp.float32) * scale
    if len(pieces) > 0:
        array = level_of(stream_key, shape, pieces, -0.22, 0.18) * array
    return jnp.clip(array, min=-most, max=most).astype(kind)


def setup_inputs(seed: int = 0) -> dict:
    key_list = jax.random.split(jax.random.key(seed), 5)
    return {
        "probes": normal_values(key_list[0], (PROBES, LEV, NLON, NLAT), 1.0, 6.0, ((2, 32), (3, 8)), jnp.float32),
        "wind": draw_wind(jax.random.fold_in(key_list[4], 71), 0),
        "wind_tend": jnp.clip(jax.random.uniform(key_list[2], (2, LEV, NLON, NLAT), jnp.float32, -0.05, 0.05) * level_of(key_list[2], (2, LEV, NLON, NLAT), ((2, 32), (3, 8)), -0.4, 0.0), -0.05, 0.05),
        "obs_weight": draw_obs_weight(jax.random.fold_in(key_list[4], 71), 0),
    }


diffuse = 0.24

def pad_grid(field):
    wrapped = jnp.concatenate((field[..., -1:, :], field, field[..., :1, :]), axis=-2)
    widths = ((0, 0),) * (field.ndim - 2) + ((0, 0), (1, 1))
    return jnp.pad(wrapped, widths)

def forward_step(field, lon_rate, lat_rate):
    east = lon_rate[..., 1:-1, 1:-1]
    north = lat_rate[..., 1:-1, 1:-1]
    middle = field[..., 1:-1, 1:-1]
    return (1.0 - 4.0 * diffuse) * middle + (diffuse - east) * field[..., 2:, 1:-1] + (diffuse + east) * field[..., :-2, 1:-1] + (diffuse - north) * field[..., 1:-1, 2:] + (diffuse + north) * field[..., 1:-1, :-2]

def adjoint_step(field, lon_rate, lat_rate):
    middle = field[..., 1:-1, 1:-1]
    return (1.0 - 4.0 * diffuse) * middle + (diffuse - lon_rate[..., :-2, 1:-1]) * field[..., :-2, 1:-1] + (diffuse + lon_rate[..., 2:, 1:-1]) * field[..., 2:, 1:-1] + (diffuse - lat_rate[..., 1:-1, :-2]) * field[..., 1:-1, :-2] + (diffuse + lat_rate[..., 1:-1, 2:]) * field[..., 1:-1, 2:]

def lower_inverse(lower):
    eye = jnp.eye(lower.shape[0], dtype=lower.dtype)
    return lax.linalg.triangular_solve(lower, eye, left_side=True, lower=True)

def reference(probes, wind, wind_tend, obs_weight):
    rates = []
    for step in range(STEPS):
        lon_rate = pad_grid(0.5 * (wind[0] + step * wind_tend[0]))
        lat_rate = pad_grid(0.5 * (wind[1] + step * wind_tend[1]))
        rates.append((lon_rate, lat_rate))

    def one_probe(field):
        for step in range(STEPS):
            field = forward_step(pad_grid(field), rates[step][0], rates[step][1])
        field = field * obs_weight
        for step in reversed(range(STEPS)):
            field = adjoint_step(pad_grid(field), rates[step][0], rates[step][1])
        return field
    hessian = lax.map(one_probe, probes)
    high = lax.Precision.HIGHEST
    gram = jnp.einsum('pabc,qabc->pq', hessian, hessian, precision=high)
    lower = jnp.linalg.cholesky(gram)
    result = jnp.einsum('pq,qabc->pabc', lower_inverse(lower), hessian, precision=high)
    upper = lower.T
    scale = jnp.sqrt(jnp.asarray(NCELLS, dtype=gram.dtype))
    return (result * scale, upper / scale)
```

```python
import jax
import jax.numpy as jnp
from jax import lax
from jax.experimental import pallas as pl
from jax.experimental.pallas import tpu as pltpu
from jax.sharding import PartitionSpec as P

STEPS = 4
HALO = 2 * STEPS

diffuse = 0.24


def lower_inverse(lower):
    eye = jnp.eye(lower.shape[0], dtype=lower.dtype)
    return lax.linalg.triangular_solve(lower, eye, left_side=True, lower=True)


def neighbours(cells, axis, dim, closed):
    count = lax.axis_size(axis)
    ends = count if closed else count - 1
    size = cells.shape[dim]
    head = lax.slice_in_dim(cells, 0, HALO, axis=dim)
    tail = lax.slice_in_dim(cells, size - HALO, size, axis=dim)
    from_next = lax.ppermute(head, axis, [((i + 1) % count, i) for i in range(ends)])
    from_prev = lax.ppermute(tail, axis, [(i, (i + 1) % count) for i in range(ends)])
    return from_next, from_prev


def shifted(x, offset, axis):
    n = x.shape[axis]
    return pltpu.roll(x, (-offset) % n, axis)


def transport_kernel(mask_ref, x_ref, o_ref, coef_ref):
    k = diffuse
    c0 = 1.0 - 4.0 * diffuse
    probes = o_ref.shape[0]
    rows = o_ref.shape[2]
    lanes = o_ref.shape[3]
    base = probes
    mask = jnp.broadcast_to(mask_ref[...], x_ref.shape[2:])
    for s in range(STEPS):
        east = 0.5 * (x_ref[0, base + 0] + s * x_ref[0, base + 2])
        north = 0.5 * (x_ref[0, base + 1] + s * x_ref[0, base + 3])
        coef_ref[s, 0] = k - east
        coef_ref[s, 1] = k + east
        coef_ref[s, 2] = k - north
        coef_ref[s, 3] = k + north
        coef_ref[s, 4] = shifted(k - east, -1, 0)
        coef_ref[s, 5] = shifted(k + east, 1, 0)
        coef_ref[s, 6] = shifted(k - north, -1, 1)
        coef_ref[s, 7] = shifted(k + north, 1, 1)

    def one_probe(p, carry):
        f = x_ref[0, p]
        for s in range(STEPS):
            f = (
                c0 * f
                + coef_ref[s, 0] * shifted(f, 1, 0)
                + coef_ref[s, 1] * shifted(f, -1, 0)
                + coef_ref[s, 2] * shifted(f, 1, 1)
                + coef_ref[s, 3] * shifted(f, -1, 1)
            )
            f = f * mask
        f = f * x_ref[0, base + 4]
        for s in reversed(range(STEPS)):
            f = (
                c0 * f
                + coef_ref[s, 4] * shifted(f, -1, 0)
                + coef_ref[s, 5] * shifted(f, 1, 0)
                + coef_ref[s, 6] * shifted(f, -1, 1)
                + coef_ref[s, 7] * shifted(f, 1, 1)
            )
            f = f * mask
        o_ref[p, 0] = f[:rows, :lanes]
        return carry

    lax.fori_loop(0, probes, one_probe, 0)


def transport(mask, stack, probes):
    levels, planes, rows, lanes = stack.shape
    out_rows = rows - 2 * HALO
    out_lanes = 128
    return pl.pallas_call(
        transport_kernel,
        grid=(levels,),
        in_specs=[
            pl.BlockSpec((1, lanes), lambda l: (0, 0)),
            pl.BlockSpec((1, planes, rows, lanes), lambda l: (l, 0, 0, 0)),
        ],
        out_specs=pl.BlockSpec((probes, 1, out_rows, out_lanes), lambda l: (0, l, 0, 0)),
        out_shape=jax.ShapeDtypeStruct((probes, levels, out_rows, out_lanes), jnp.float32),
        scratch_shapes=[pltpu.VMEM((STEPS, 8, rows, lanes), jnp.float32)],
    )(mask, stack)


def body(probes, wind, wind_tend, obs_weight):
    n_probes, levels, width_lon, width_lat = probes.shape
    stack = jnp.concatenate(
        (
            jnp.swapaxes(probes, 0, 1),
            jnp.swapaxes(wind, 0, 1),
            jnp.swapaxes(wind_tend, 0, 1),
            obs_weight[:, None],
        ),
        axis=1,
    )
    lon_next, lon_prev = neighbours(stack, "lon", 2, True)
    stack = jnp.concatenate((stack, lon_next, lon_prev), axis=2)
    lat_in = jnp.swapaxes(stack, 2, 3)
    lat_next, lat_prev = neighbours(lat_in, "lat", 2, False)
    lanes = 256
    gap = jnp.zeros(stack.shape[:3] + (lanes - width_lat - 2 * HALO,), stack.dtype)
    stack = jnp.concatenate(
        (stack, jnp.swapaxes(lat_next, 2, 3), gap, jnp.swapaxes(lat_prev, 2, 3)), axis=3
    )
    lane = lax.broadcasted_iota(jnp.int32, (1, lanes), 1)
    start = lax.axis_index("lat") * width_lat
    cell = jnp.where(lane < width_lat + HALO, start + lane, start + lane - lanes)
    inside = ((lane < width_lat + HALO) | (lane >= lanes - HALO)) & (cell >= 0)
    inside = inside & (cell < width_lat * lax.axis_size("lat"))
    mask = inside.astype(jnp.float32)

    field = transport(mask, stack, n_probes)

    high = lax.Precision.HIGHEST
    flat = field.reshape(field.shape[0], -1)
    gram = lax.psum(jnp.einsum("pc,qc->pq", flat, flat, precision=high), ("lat", "lon"))
    lower = jnp.linalg.cholesky(gram)
    result = jnp.dot(lower_inverse(lower), flat, precision=high)
    upper = lower.T
    cells = field.shape[1] * width_lon * width_lat * lax.axis_size("lat") * lax.axis_size("lon")
    scale = jnp.sqrt(jnp.float32(cells))
    return ((result * scale).reshape(field.shape), upper / scale)


def solution(mesh):
    placed = (
        P(None, None, "lon", "lat"),
        P(None, None, "lon", "lat"),
        P(None, None, "lon", "lat"),
        P(None, "lon", "lat"),
    )
    return jax.shard_map(
        body,
        mesh=mesh,
        in_specs=placed,
        out_specs=(P(None, None, "lon", "lat"), P()),
        check_vma=False,
    )
```

```python
import jax
import jax.numpy as jnp
from jax import lax
from jax.experimental import pallas as pl
from jax.experimental.pallas import tpu as pltpu
from jax.sharding import PartitionSpec as P

STEPS = 4
HALO = 2 * STEPS

diffuse = 0.24


def lower_inverse(lower):
    eye = jnp.eye(lower.shape[0], dtype=lower.dtype)
    return lax.linalg.triangular_solve(lower, eye, left_side=True, lower=True)


def all_sum(value, axes):
    for axis in axes:
        count = lax.axis_size(axis)
        if count & (count - 1):
            value = lax.psum(value, axis)
            continue
        stride = 1
        while stride < count:
            value = value + lax.ppermute(value, axis, [(i, i ^ stride) for i in range(count)])
            stride *= 2
    return value


def neighbours(cells, axis, dim, closed):
    count = lax.axis_size(axis)
    ends = count if closed else count - 1
    size = cells.shape[dim]
    head = lax.slice_in_dim(cells, 0, HALO, axis=dim)
    tail = lax.slice_in_dim(cells, size - HALO, size, axis=dim)
    from_next = lax.ppermute(head, axis, [((i + 1) % count, i) for i in range(ends)])
    from_prev = lax.ppermute(tail, axis, [(i, (i + 1) % count) for i in range(ends)])
    return from_next, from_prev


def shifted(x, offset, axis):
    n = x.shape[axis]
    return pltpu.roll(x, (-offset) % n, axis)


def transport_kernel(mask_ref, x_ref, o_ref, coef_ref):
    k = diffuse
    c0 = 1.0 - 4.0 * diffuse
    probes = o_ref.shape[0]
    rows = o_ref.shape[2]
    lanes = o_ref.shape[3]
    base = probes
    mask = jnp.broadcast_to(mask_ref[...], x_ref.shape[2:])
    for s in range(STEPS):
        east = 0.5 * (x_ref[0, base + 0] + s * x_ref[0, base + 2])
        north = 0.5 * (x_ref[0, base + 1] + s * x_ref[0, base + 3])
        coef_ref[s, 0] = k - east
        coef_ref[s, 1] = k + east
        coef_ref[s, 2] = k - north
        coef_ref[s, 3] = k + north
        coef_ref[s, 4] = shifted(k - east, -1, 0)
        coef_ref[s, 5] = shifted(k + east, 1, 0)
        coef_ref[s, 6] = shifted(k - north, -1, 1)
        coef_ref[s, 7] = shifted(k + north, 1, 1)

    def one_probe(p, carry):
        f = x_ref[0, p]
        for s in range(STEPS):
            f = (
                c0 * f
                + coef_ref[s, 0] * shifted(f, 1, 0)
                + coef_ref[s, 1] * shifted(f, -1, 0)
                + coef_ref[s, 2] * shifted(f, 1, 1)
                + coef_ref[s, 3] * shifted(f, -1, 1)
            )
            f = f * mask
        f = f * x_ref[0, base + 4]
        for s in reversed(range(STEPS)):
            f = (
                c0 * f
                + coef_ref[s, 4] * shifted(f, -1, 0)
                + coef_ref[s, 5] * shifted(f, 1, 0)
                + coef_ref[s, 6] * shifted(f, -1, 1)
                + coef_ref[s, 7] * shifted(f, 1, 1)
            )
            f = f * mask
        o_ref[p, 0] = f[:rows, :lanes]
        return carry

    lax.fori_loop(0, probes, one_probe, 0)


def transport(mask, stack, probes):
    levels, planes, rows, lanes = stack.shape
    out_rows = rows - 2 * HALO
    out_lanes = 128
    return pl.pallas_call(
        transport_kernel,
        grid=(levels,),
        in_specs=[
            pl.BlockSpec((1, lanes), lambda l: (0, 0)),
            pl.BlockSpec((1, planes, rows, lanes), lambda l: (l, 0, 0, 0)),
        ],
        out_specs=pl.BlockSpec((probes, 1, out_rows, out_lanes), lambda l: (0, l, 0, 0)),
        out_shape=jax.ShapeDtypeStruct((probes, levels, out_rows, out_lanes), jnp.float32),
        scratch_shapes=[pltpu.VMEM((STEPS, 8, rows, lanes), jnp.float32)],
    )(mask, stack)


def body(probes, wind, wind_tend, obs_weight):
    n_probes, levels, width_lon, width_lat = probes.shape
    stack = jnp.concatenate(
        (
            jnp.swapaxes(probes, 0, 1),
            jnp.swapaxes(wind, 0, 1),
            jnp.swapaxes(wind_tend, 0, 1),
            obs_weight[:, None],
        ),
        axis=1,
    )
    lon_next, lon_prev = neighbours(stack, "lon", 2, True)
    stack = jnp.concatenate((stack, lon_next, lon_prev), axis=2)
    lat_in = jnp.swapaxes(stack, 2, 3)
    lat_next, lat_prev = neighbours(lat_in, "lat", 2, False)
    lanes = 256
    gap = jnp.zeros(stack.shape[:3] + (lanes - width_lat - 2 * HALO,), stack.dtype)
    stack = jnp.concatenate(
        (stack, jnp.swapaxes(lat_next, 2, 3), gap, jnp.swapaxes(lat_prev, 2, 3)), axis=3
    )
    lane = lax.broadcasted_iota(jnp.int32, (1, lanes), 1)
    start = lax.axis_index("lat") * width_lat
    cell = jnp.where(lane < width_lat + HALO, start + lane, start + lane - lanes)
    inside = ((lane < width_lat + HALO) | (lane >= lanes - HALO)) & (cell >= 0)
    inside = inside & (cell < width_lat * lax.axis_size("lat"))
    mask = inside.astype(jnp.float32)

    field = transport(mask, stack, n_probes)

    high = lax.Precision.HIGHEST
    flat = field.reshape(field.shape[0], -1)
    gram = all_sum(jnp.einsum("pc,qc->pq", flat, flat, precision=high), ("lon", "lat"))
    lower = jnp.linalg.cholesky(gram)
    result = jnp.dot(lower_inverse(lower), flat, precision=high)
    upper = lower.T
    cells = field.shape[1] * width_lon * width_lat * lax.axis_size("lat") * lax.axis_size("lon")
    scale = jnp.sqrt(jnp.float32(cells))
    return ((result * scale).reshape(field.shape), upper / scale)


def solution(mesh):
    placed = (
        P(None, None, "lon", "lat"),
        P(None, None, "lon", "lat"),
        P(None, None, "lon", "lat"),
        P(None, "lon", "lat"),
    )
    return jax.shard_map(
        body,
        mesh=mesh,
        in_specs=placed,
        out_specs=(P(None, None, "lon", "lat"), P()),
        check_vma=False,
    )
```

```python
import jax
import jax.numpy as jnp
from jax import lax
from jax.experimental import pallas as pl
from jax.experimental.pallas import tpu as pltpu
from jax.sharding import PartitionSpec as P

STEPS = 4
HALO = 2 * STEPS

diffuse = 0.24


def lower_inverse(lower):
    eye = jnp.eye(lower.shape[0], dtype=lower.dtype)
    return lax.linalg.triangular_solve(lower, eye, left_side=True, lower=True)


def all_sum(value, axes):
    for axis in axes:
        count = lax.axis_size(axis)
        if count & (count - 1):
            value = lax.psum(value, axis)
            continue
        stride = 1
        while stride < count:
            value = value + lax.ppermute(value, axis, [(i, i ^ stride) for i in range(count)])
            stride *= 2
    return value


def neighbours(cells, axis, dim, closed):
    count = lax.axis_size(axis)
    ends = count if closed else count - 1
    size = cells.shape[dim]
    head = lax.slice_in_dim(cells, 0, HALO, axis=dim)
    tail = lax.slice_in_dim(cells, size - HALO, size, axis=dim)
    from_next = lax.ppermute(head, axis, [((i + 1) % count, i) for i in range(ends)])
    from_prev = lax.ppermute(tail, axis, [(i, (i + 1) % count) for i in range(ends)])
    return from_next, from_prev


def shifted(x, offset, axis):
    n = x.shape[axis]
    return pltpu.roll(x, (-offset) % n, axis)


def transport_kernel(mask_ref, x_ref, o_ref, g_ref, coef_ref):
    k = diffuse
    c0 = 1.0 - 4.0 * diffuse
    probes = o_ref.shape[0]
    rows = o_ref.shape[2]
    lanes = o_ref.shape[3]
    base = probes
    mask = jnp.broadcast_to(mask_ref[...], x_ref.shape[2:])
    for s in range(STEPS):
        east = 0.5 * (x_ref[0, base + 0] + s * x_ref[0, base + 2])
        north = 0.5 * (x_ref[0, base + 1] + s * x_ref[0, base + 3])
        coef_ref[s, 0] = k - east
        coef_ref[s, 1] = k + east
        coef_ref[s, 2] = k - north
        coef_ref[s, 3] = k + north
        coef_ref[s, 4] = shifted(k - east, -1, 0)
        coef_ref[s, 5] = shifted(k + east, 1, 0)
        coef_ref[s, 6] = shifted(k - north, -1, 1)
        coef_ref[s, 7] = shifted(k + north, 1, 1)

    def one_probe(p, carry):
        f = x_ref[0, p]
        for s in range(STEPS):
            f = (
                c0 * f
                + coef_ref[s, 0] * shifted(f, 1, 0)
                + coef_ref[s, 1] * shifted(f, -1, 0)
                + coef_ref[s, 2] * shifted(f, 1, 1)
                + coef_ref[s, 3] * shifted(f, -1, 1)
            )
            f = f * mask
        f = f * x_ref[0, base + 4]
        for s in reversed(range(STEPS)):
            f = (
                c0 * f
                + coef_ref[s, 4] * shifted(f, -1, 0)
                + coef_ref[s, 5] * shifted(f, 1, 0)
                + coef_ref[s, 6] * shifted(f, -1, 1)
                + coef_ref[s, 7] * shifted(f, 1, 1)
            )
            f = f * mask
        o_ref[p, 0] = f[:rows, :lanes]
        return carry

    lax.fori_loop(0, probes, one_probe, 0)
    for p in range(probes):
        for q in range(p, probes):
            prod = (o_ref[p, 0] * o_ref[q, 0]).reshape(rows // 8, 8, lanes)
            part = jnp.sum(jnp.sum(prod, axis=0), axis=0, keepdims=True)
            g_ref[0, pl.ds(p * probes + q, 1), :] = part
            if q != p:
                g_ref[0, pl.ds(q * probes + p, 1), :] = part


def transport(mask, stack, probes):
    levels, planes, rows, lanes = stack.shape
    out_rows = rows - 2 * HALO
    out_lanes = 128
    return pl.pallas_call(
        transport_kernel,
        grid=(levels,),
        in_specs=[
            pl.BlockSpec((1, lanes), lambda l: (0, 0)),
            pl.BlockSpec((1, planes, rows, lanes), lambda l: (l, 0, 0, 0)),
        ],
        out_specs=[
            pl.BlockSpec((probes, 1, out_rows, out_lanes), lambda l: (0, l, 0, 0)),
            pl.BlockSpec((1, probes * probes, out_lanes), lambda l: (l, 0, 0)),
        ],
        out_shape=[
            jax.ShapeDtypeStruct((probes, levels, out_rows, out_lanes), jnp.float32),
            jax.ShapeDtypeStruct((levels, probes * probes, out_lanes), jnp.float32),
        ],
        scratch_shapes=[pltpu.VMEM((STEPS, 8, rows, lanes), jnp.float32)],
    )(mask, stack)


def basis_kernel(inv_ref, scale_ref, z_ref, o_ref):
    probes = z_ref.shape[0]
    z = [z_ref[q, 0] for q in range(probes)]
    for p in range(probes):
        acc = inv_ref[p, 0] * z[0]
        for q in range(1, probes):
            acc = acc + inv_ref[p, q] * z[q]
        o_ref[p, 0] = acc * scale_ref[0, 0]


def basis(inverse, scale, field):
    probes, levels, rows, lanes = field.shape
    block = pl.BlockSpec((probes, 1, rows, lanes), lambda l: (0, l, 0, 0))
    return pl.pallas_call(
        basis_kernel,
        grid=(levels,),
        in_specs=[
            pl.BlockSpec(memory_space=pltpu.SMEM),
            pl.BlockSpec(memory_space=pltpu.SMEM),
            block,
        ],
        out_specs=block,
        out_shape=jax.ShapeDtypeStruct(field.shape, jnp.float32),
    )(inverse, scale, field)


def body(probes, wind, wind_tend, obs_weight):
    n_probes, levels, width_lon, width_lat = probes.shape
    stack = jnp.concatenate(
        (
            jnp.swapaxes(probes, 0, 1),
            jnp.swapaxes(wind, 0, 1),
            jnp.swapaxes(wind_tend, 0, 1),
            obs_weight[:, None],
        ),
        axis=1,
    )
    lon_next, lon_prev = neighbours(stack, "lon", 2, True)
    stack = jnp.concatenate((stack, lon_next, lon_prev), axis=2)
    lat_in = jnp.swapaxes(stack, 2, 3)
    lat_next, lat_prev = neighbours(lat_in, "lat", 2, False)
    lanes = 256
    gap = jnp.zeros(stack.shape[:3] + (lanes - width_lat - 2 * HALO,), stack.dtype)
    stack = jnp.concatenate(
        (stack, jnp.swapaxes(lat_next, 2, 3), gap, jnp.swapaxes(lat_prev, 2, 3)), axis=3
    )
    lane = lax.broadcasted_iota(jnp.int32, (1, lanes), 1)
    start = lax.axis_index("lat") * width_lat
    cell = jnp.where(lane < width_lat + HALO, start + lane, start + lane - lanes)
    inside = ((lane < width_lat + HALO) | (lane >= lanes - HALO)) & (cell >= 0)
    inside = inside & (cell < width_lat * lax.axis_size("lat"))
    mask = inside.astype(jnp.float32)

    field, partial = transport(mask, stack, n_probes)

    gram = jnp.sum(partial, axis=(0, 2)).reshape(n_probes, n_probes)
    gram = all_sum(gram, ("lon", "lat"))
    lower = jnp.linalg.cholesky(gram)
    upper = lower.T
    cells = field.shape[1] * width_lon * width_lat * lax.axis_size("lat") * lax.axis_size("lon")
    scale = jnp.sqrt(jnp.float32(cells))
    result = basis(lower_inverse(lower), scale.reshape(1, 1), field)
    return (result, upper / scale)


def solution(mesh):
    placed = (
        P(None, None, "lon", "lat"),
        P(None, None, "lon", "lat"),
        P(None, None, "lon", "lat"),
        P(None, "lon", "lat"),
    )
    return jax.shard_map(
        body,
        mesh=mesh,
        in_specs=placed,
        out_specs=(P(None, None, "lon", "lat"), P()),
        check_vma=False,
    )
```

```python
import jax
import jax.numpy as jnp
from jax import lax
from jax.experimental import pallas as pl
from jax.experimental.pallas import tpu as pltpu
from jax.sharding import PartitionSpec as P

STEPS = 4
HALO = 2 * STEPS

diffuse = 0.24


def lower_inverse(lower):
    eye = jnp.eye(lower.shape[0], dtype=lower.dtype)
    return lax.linalg.triangular_solve(lower, eye, left_side=True, lower=True)


def all_sum(value, axes):
    for axis in axes:
        count = lax.axis_size(axis)
        if count & (count - 1):
            value = lax.psum(value, axis)
            continue
        stride = 1
        while stride < count:
            value = value + lax.ppermute(value, axis, [(i, i ^ stride) for i in range(count)])
            stride *= 2
    return value


def neighbours(cells, axis, dim, closed):
    count = lax.axis_size(axis)
    ends = count if closed else count - 1
    size = cells.shape[dim]
    head = lax.slice_in_dim(cells, 0, HALO, axis=dim)
    tail = lax.slice_in_dim(cells, size - HALO, size, axis=dim)
    from_next = lax.ppermute(head, axis, [((i + 1) % count, i) for i in range(ends)])
    from_prev = lax.ppermute(tail, axis, [(i, (i + 1) % count) for i in range(ends)])
    return from_next, from_prev


def shifted(x, offset, axis):
    n = x.shape[axis]
    return pltpu.roll(x, (-offset) % n, axis)


def transport_kernel(mask_ref, x_ref, o_ref, g_ref, coef_ref):
    k = diffuse
    c0 = 1.0 - 4.0 * diffuse
    probes = o_ref.shape[0]
    rows = o_ref.shape[2]
    lanes = o_ref.shape[3]
    base = probes
    mask = jnp.broadcast_to(mask_ref[...], x_ref.shape[2:])
    for s in range(STEPS):
        east = 0.5 * (x_ref[0, base + 0] + s * x_ref[0, base + 2])
        north = 0.5 * (x_ref[0, base + 1] + s * x_ref[0, base + 3])
        coef_ref[s, 0] = k - east
        coef_ref[s, 1] = k + east
        coef_ref[s, 2] = k - north
        coef_ref[s, 3] = k + north
        coef_ref[s, 4] = shifted(k - east, -1, 0)
        coef_ref[s, 5] = shifted(k + east, 1, 0)
        coef_ref[s, 6] = shifted(k - north, -1, 1)
        coef_ref[s, 7] = shifted(k + north, 1, 1)

    def one_probe(p, carry):
        f = x_ref[0, p]
        for s in range(STEPS):
            f = (
                c0 * f
                + coef_ref[s, 0] * shifted(f, 1, 0)
                + coef_ref[s, 1] * shifted(f, -1, 0)
                + coef_ref[s, 2] * shifted(f, 1, 1)
                + coef_ref[s, 3] * shifted(f, -1, 1)
            )
            f = f * mask
        f = f * x_ref[0, base + 4]
        for s in reversed(range(STEPS)):
            f = (
                c0 * f
                + coef_ref[s, 4] * shifted(f, -1, 0)
                + coef_ref[s, 5] * shifted(f, 1, 0)
                + coef_ref[s, 6] * shifted(f, -1, 1)
                + coef_ref[s, 7] * shifted(f, 1, 1)
            )
            f = f * mask
        o_ref[p, 0] = f[:rows, :lanes]
        return carry

    lax.fori_loop(0, probes, one_probe, 0)
    for p in range(probes):
        for q in range(p, probes):
            prod = (o_ref[p, 0] * o_ref[q, 0]).reshape(rows // 8, 8, lanes)
            part = jnp.sum(jnp.sum(prod, axis=0), axis=0, keepdims=True)
            g_ref[0, pl.ds(p * probes + q, 1), :] = part
            if q != p:
                g_ref[0, pl.ds(q * probes + p, 1), :] = part


def transport(mask, stack, probes):
    levels, planes, rows, lanes = stack.shape
    out_rows = rows - 2 * HALO
    out_lanes = 128
    return pl.pallas_call(
        transport_kernel,
        grid=(levels,),
        in_specs=[
            pl.BlockSpec((1, lanes), lambda l: (0, 0)),
            pl.BlockSpec((1, planes, rows, lanes), lambda l: (l, 0, 0, 0)),
        ],
        out_specs=[
            pl.BlockSpec((probes, 1, out_rows, out_lanes), lambda l: (0, l, 0, 0)),
            pl.BlockSpec((1, probes * probes, out_lanes), lambda l: (l, 0, 0)),
        ],
        out_shape=[
            jax.ShapeDtypeStruct((probes, levels, out_rows, out_lanes), jnp.float32),
            jax.ShapeDtypeStruct((levels, probes * probes, out_lanes), jnp.float32),
        ],
        scratch_shapes=[pltpu.VMEM((STEPS, 8, rows, lanes), jnp.float32)],
    )(mask, stack)


def basis_kernel(inv_ref, scale_ref, z_ref, o_ref):
    probes = z_ref.shape[0]
    z = [z_ref[q, 0] for q in range(probes)]
    for p in range(probes):
        acc = inv_ref[p, 0] * z[0]
        for q in range(1, probes):
            acc = acc + inv_ref[p, q] * z[q]
        o_ref[p, 0] = acc * scale_ref[0, 0]


def basis(inverse, scale, field):
    probes, levels, rows, lanes = field.shape
    block = pl.BlockSpec((probes, 1, rows, lanes), lambda l: (0, l, 0, 0))
    return pl.pallas_call(
        basis_kernel,
        grid=(levels,),
        in_specs=[
            pl.BlockSpec(memory_space=pltpu.SMEM),
            pl.BlockSpec(memory_space=pltpu.SMEM),
            block,
        ],
        out_specs=block,
        out_shape=jax.ShapeDtypeStruct(field.shape, jnp.float32),
    )(inverse, scale, field)


def body(probes, wind, wind_tend, obs_weight):
    n_probes, levels, width_lon, width_lat = probes.shape
    stack = jnp.concatenate(
        (
            jnp.swapaxes(probes, 0, 1),
            jnp.swapaxes(wind, 0, 1),
            jnp.swapaxes(wind_tend, 0, 1),
            obs_weight[:, None],
        ),
        axis=1,
    )
    n_lon = lax.axis_size("lon")
    n_lat = lax.axis_size("lat")
    head_rows = stack[:, :, :HALO]
    tail_rows = stack[:, :, width_lon - HALO :]

    def lat_edges(rows):
        return jnp.swapaxes(rows[..., :HALO], 2, 3), jnp.swapaxes(rows[..., width_lat - HALO :], 2, 3)

    def lon_send(x, up):
        pairs = [((i + 1) % n_lon, i) if up else (i, (i + 1) % n_lon) for i in range(n_lon)]
        return lax.ppermute(x, "lon", pairs)

    def lat_send(x, up):
        pairs = [(j + 1, j) if up else (j, j + 1) for j in range(n_lat - 1)]
        return lax.ppermute(x, "lat", pairs)

    def diagonal_send(x, lon_up, lat_up):
        pairs = []
        for i in range(n_lon):
            for j in range(n_lat - 1):
                ni = (i + 1) % n_lon
                src_i, dst_i = (ni, i) if lon_up else (i, ni)
                src_j, dst_j = (j + 1, j) if lat_up else (j, j + 1)
                pairs.append((src_j * n_lon + src_i, dst_j * n_lon + dst_i))
        return lax.ppermute(x, ("lat", "lon"), pairs)

    own_head, own_tail = lat_edges(stack)
    lon_next = lon_send(head_rows, True)
    lon_prev = lon_send(tail_rows, False)
    lat_next = lat_send(own_head, True)
    lat_prev = lat_send(own_tail, False)
    corner_nn = diagonal_send(head_rows[..., :HALO], True, True)
    corner_np = diagonal_send(head_rows[..., width_lat - HALO :], True, False)
    corner_pn = diagonal_send(tail_rows[..., :HALO], False, True)
    corner_pp = diagonal_send(tail_rows[..., width_lat - HALO :], False, False)
    lanes = 256
    gap = jnp.zeros(stack.shape[:2] + (width_lon + 2 * HALO, lanes - width_lat - 2 * HALO), stack.dtype)
    left = jnp.concatenate((stack, lon_next, lon_prev), axis=2)
    right_next = jnp.concatenate((jnp.swapaxes(lat_next, 2, 3), corner_nn, corner_pn), axis=2)
    right_prev = jnp.concatenate((jnp.swapaxes(lat_prev, 2, 3), corner_np, corner_pp), axis=2)
    stack = jnp.concatenate((left, right_next, gap, right_prev), axis=3)
    lane = lax.broadcasted_iota(jnp.int32, (1, lanes), 1)
    start = lax.axis_index("lat") * width_lat
    cell = jnp.where(lane < width_lat + HALO, start + lane, start + lane - lanes)
    inside = ((lane < width_lat + HALO) | (lane >= lanes - HALO)) & (cell >= 0)
    inside = inside & (cell < width_lat * lax.axis_size("lat"))
    mask = inside.astype(jnp.float32)

    field, partial = transport(mask, stack, n_probes)

    gram = jnp.sum(partial, axis=(0, 2)).reshape(n_probes, n_probes)
    gram = all_sum(gram, ("lon", "lat"))
    lower = jnp.linalg.cholesky(gram)
    upper = lower.T
    cells = field.shape[1] * width_lon * width_lat * lax.axis_size("lat") * lax.axis_size("lon")
    scale = jnp.sqrt(jnp.float32(cells))
    result = basis(lower_inverse(lower), scale.reshape(1, 1), field)
    return (result, upper / scale)


def solution(mesh):
    placed = (
        P(None, None, "lon", "lat"),
        P(None, None, "lon", "lat"),
        P(None, None, "lon", "lat"),
        P(None, "lon", "lat"),
    )
    return jax.shard_map(
        body,
        mesh=mesh,
        in_specs=placed,
        out_specs=(P(None, None, "lon", "lat"), P()),
        check_vma=False,
    )
```

```python
import jax
import jax.numpy as jnp
from jax import lax
from jax.experimental import pallas as pl
from jax.experimental.pallas import tpu as pltpu
from jax.sharding import PartitionSpec as P

STEPS = 4
HALO = 2 * STEPS

diffuse = 0.24


def lower_inverse(lower):
    eye = jnp.eye(lower.shape[0], dtype=lower.dtype)
    return lax.linalg.triangular_solve(lower, eye, left_side=True, lower=True)


def all_sum(value, axes):
    for axis in axes:
        count = lax.axis_size(axis)
        if count & (count - 1):
            value = lax.psum(value, axis)
            continue
        stride = 1
        while stride < count:
            value = value + lax.ppermute(value, axis, [(i, i ^ stride) for i in range(count)])
            stride *= 2
    return value


def shifted(x, offset, axis):
    n = x.shape[axis]
    return pltpu.roll(x, (-offset) % n, axis)


def transport_kernel(
    mask_ref, pr_ref, wi_ref, te_ref, ob_ref, ln_ref, lp_ref, rt_ref, o_ref, g_ref, coef_ref, plane_ref
):
    k = diffuse
    c0 = 1.0 - 4.0 * diffuse
    probes = o_ref.shape[0]
    rows = o_ref.shape[2]
    lanes = o_ref.shape[3]
    full_rows, full_lanes = plane_ref.shape
    mask = mask_ref[...]

    def masked(f):
        return (f.reshape(full_rows // 8, 8, full_lanes) * mask[None]).reshape(full_rows, full_lanes)

    def assemble(own, plane):
        plane_ref[0:rows, 0:lanes] = own
        plane_ref[rows : rows + HALO, 0:lanes] = ln_ref[0, plane]
        plane_ref[rows + HALO : full_rows, 0:lanes] = lp_ref[0, plane]
        plane_ref[:, lanes:full_lanes] = rt_ref[0, plane]
        return plane_ref[...]

    w_east = assemble(wi_ref[0, 0], probes + 0)
    w_north = assemble(wi_ref[1, 0], probes + 1)
    t_east = assemble(te_ref[0, 0], probes + 2)
    t_north = assemble(te_ref[1, 0], probes + 3)
    for s in range(STEPS):
        east = 0.5 * (w_east + s * t_east)
        north = 0.5 * (w_north + s * t_north)
        coef_ref[s, 0] = k - east
        coef_ref[s, 1] = k + east
        coef_ref[s, 2] = k - north
        coef_ref[s, 3] = k + north
        coef_ref[s, 4] = shifted(k - east, -1, 0)
        coef_ref[s, 5] = shifted(k + east, 1, 0)
        coef_ref[s, 6] = shifted(k - north, -1, 1)
        coef_ref[s, 7] = shifted(k + north, 1, 1)
    coef_ref[STEPS, 0] = assemble(ob_ref[0], probes + 4)

    def one_probe(p, carry):
        f = assemble(pr_ref[p, 0], p)
        for s in range(STEPS):
            f = (
                c0 * f
                + coef_ref[s, 0] * shifted(f, 1, 0)
                + coef_ref[s, 1] * shifted(f, -1, 0)
                + coef_ref[s, 2] * shifted(f, 1, 1)
                + coef_ref[s, 3] * shifted(f, -1, 1)
            )
            f = masked(f)
        f = f * coef_ref[STEPS, 0]
        for s in reversed(range(STEPS)):
            f = (
                c0 * f
                + coef_ref[s, 4] * shifted(f, -1, 0)
                + coef_ref[s, 5] * shifted(f, 1, 0)
                + coef_ref[s, 6] * shifted(f, -1, 1)
                + coef_ref[s, 7] * shifted(f, 1, 1)
            )
            f = masked(f)
        o_ref[p, 0] = f[:rows, :lanes]
        return carry

    lax.fori_loop(0, probes, one_probe, 0)
    for p in range(probes):
        for q in range(p, probes):
            prod = (o_ref[p, 0] * o_ref[q, 0]).reshape(rows // 8, 8, lanes)
            part = jnp.sum(jnp.sum(prod, axis=0), axis=0, keepdims=True)
            g_ref[0, pl.ds(p * probes + q, 1), :] = part
            if q != p:
                g_ref[0, pl.ds(q * probes + p, 1), :] = part


def transport(mask, probes, wind, wind_tend, obs_weight, lon_next, lon_prev, lat_block):
    n_probes, levels, rows, lanes = probes.shape
    planes = lon_next.shape[1]
    full_rows = rows + 2 * HALO
    full_lanes = 2 * lanes

    def level_block(lead):
        return pl.BlockSpec((lead, 1, rows, lanes), lambda l: (0, l, 0, 0))

    def halo_block(height):
        return pl.BlockSpec((1, planes, height, lanes), lambda l: (l, 0, 0, 0))

    return pl.pallas_call(
        transport_kernel,
        grid=(levels,),
        in_specs=[
            pl.BlockSpec((8, full_lanes), lambda l: (0, 0)),
            level_block(n_probes),
            level_block(2),
            level_block(2),
            pl.BlockSpec((1, rows, lanes), lambda l: (l, 0, 0)),
            halo_block(HALO),
            halo_block(HALO),
            halo_block(full_rows),
        ],
        out_specs=[
            level_block(n_probes),
            pl.BlockSpec((1, n_probes * n_probes, lanes), lambda l: (l, 0, 0)),
        ],
        out_shape=[
            jax.ShapeDtypeStruct((n_probes, levels, rows, lanes), jnp.float32),
            jax.ShapeDtypeStruct((levels, n_probes * n_probes, lanes), jnp.float32),
        ],
        scratch_shapes=[
            pltpu.VMEM((STEPS + 1, 8, full_rows, full_lanes), jnp.float32),
            pltpu.VMEM((full_rows, full_lanes), jnp.float32),
        ],
    )(mask, probes, wind, wind_tend, obs_weight, lon_next, lon_prev, lat_block)

def basis_kernel(inv_ref, scale_ref, z_ref, o_ref):
    probes = z_ref.shape[0]
    z = [z_ref[q, 0] for q in range(probes)]
    for p in range(probes):
        acc = inv_ref[p, 0] * z[0]
        for q in range(1, probes):
            acc = acc + inv_ref[p, q] * z[q]
        o_ref[p, 0] = acc * scale_ref[0, 0]


def basis(inverse, scale, field):
    probes, levels, rows, lanes = field.shape
    block = pl.BlockSpec((probes, 1, rows, lanes), lambda l: (0, l, 0, 0))
    return pl.pallas_call(
        basis_kernel,
        grid=(levels,),
        in_specs=[
            pl.BlockSpec(memory_space=pltpu.SMEM),
            pl.BlockSpec(memory_space=pltpu.SMEM),
            block,
        ],
        out_specs=block,
        out_shape=jax.ShapeDtypeStruct(field.shape, jnp.float32),
    )(inverse, scale, field)


def body(probes, wind, wind_tend, obs_weight):
    n_probes, levels, width_lon, width_lat = probes.shape

    def planes_of(part):
        return jnp.concatenate(
            (
                jnp.swapaxes(part(probes), 0, 1),
                jnp.swapaxes(part(wind), 0, 1),
                jnp.swapaxes(part(wind_tend), 0, 1),
                part(obs_weight[None])[0][:, None],
            ),
            axis=1,
        )

    heads = planes_of(lambda a: a[..., :HALO, :])
    tails = planes_of(lambda a: a[..., width_lon - HALO :, :])
    n_lon = lax.axis_size("lon")
    lon_next = lax.ppermute(heads, "lon", [((i + 1) % n_lon, i) for i in range(n_lon)])
    lon_prev = lax.ppermute(tails, "lon", [(i, (i + 1) % n_lon) for i in range(n_lon)])
    own_lo = planes_of(lambda a: a[..., :HALO])
    own_hi = planes_of(lambda a: a[..., width_lat - HALO :])
    edge_lo = jnp.concatenate((own_lo, lon_next[..., :HALO], lon_prev[..., :HALO]), axis=2)
    edge_hi = jnp.concatenate(
        (own_hi, lon_next[..., width_lat - HALO :], lon_prev[..., width_lat - HALO :]), axis=2
    )
    n_lat = lax.axis_size("lat")
    lat_next = lax.ppermute(jnp.swapaxes(edge_lo, 2, 3), "lat", [(j + 1, j) for j in range(n_lat - 1)])
    lat_prev = lax.ppermute(jnp.swapaxes(edge_hi, 2, 3), "lat", [(j, j + 1) for j in range(n_lat - 1)])
    gap = jnp.zeros(edge_lo.shape[:3] + (width_lat - 2 * HALO,), jnp.float32)
    lat_block = jnp.concatenate(
        (jnp.swapaxes(lat_next, 2, 3), gap, jnp.swapaxes(lat_prev, 2, 3)), axis=3
    )
    lanes = 2 * width_lat
    lane = lax.broadcasted_iota(jnp.int32, (8, lanes), 1)
    start = lax.axis_index("lat") * width_lat
    cell = jnp.where(lane < width_lat + HALO, start + lane, start + lane - lanes)
    inside = ((lane < width_lat + HALO) | (lane >= lanes - HALO)) & (cell >= 0)
    inside = inside & (cell < width_lat * n_lat)
    mask = inside.astype(jnp.float32)

    field, partial = transport(
        mask, probes, wind, wind_tend, obs_weight, lon_next, lon_prev, lat_block
    )

    gram = jnp.sum(partial, axis=(0, 2)).reshape(n_probes, n_probes)
    gram = all_sum(gram, ("lon", "lat"))
    lower = jnp.linalg.cholesky(gram)
    upper = lower.T
    cells = field.shape[1] * width_lon * width_lat * lax.axis_size("lat") * lax.axis_size("lon")
    scale = jnp.sqrt(jnp.float32(cells))
    result = basis(lower_inverse(lower), scale.reshape(1, 1), field)
    return (result, upper / scale)


def solution(mesh):
    placed = (
        P(None, None, "lon", "lat"),
        P(None, None, "lon", "lat"),
        P(None, None, "lon", "lat"),
        P(None, "lon", "lat"),
    )
    return jax.shard_map(
        body,
        mesh=mesh,
        in_specs=placed,
        out_specs=(P(None, None, "lon", "lat"), P()),
        check_vma=False,
    )
```

```python
import jax
import jax.numpy as jnp
from jax import lax
from jax.experimental import pallas as pl
from jax.experimental.pallas import tpu as pltpu
from jax.sharding import PartitionSpec as P

STEPS = 4
HALO = 2 * STEPS

diffuse = 0.24


def lower_inverse(lower):
    eye = jnp.eye(lower.shape[0], dtype=lower.dtype)
    return lax.linalg.triangular_solve(lower, eye, left_side=True, lower=True)


def all_sum(value, axes):
    for axis in axes:
        count = lax.axis_size(axis)
        if count & (count - 1):
            value = lax.psum(value, axis)
            continue
        stride = 1
        while stride < count:
            value = value + lax.ppermute(value, axis, [(i, i ^ stride) for i in range(count)])
            stride *= 2
    return value


def shifted(x, offset, axis):
    n = x.shape[axis]
    return pltpu.roll(x, (-offset) % n, axis)


def transport_kernel(
    mask_ref, pr_ref, wi_ref, te_ref, ob_ref, ln_ref, lp_ref, rt_ref, o_ref, g_ref, coef_ref, plane_ref
):
    k = diffuse
    c0 = 1.0 - 4.0 * diffuse
    probes = o_ref.shape[0]
    rows = o_ref.shape[2]
    lanes = o_ref.shape[3]
    full_rows, full_lanes = plane_ref.shape[1:]
    mask = mask_ref[...]

    def masked(f):
        return (f.reshape(full_rows // 8, 8, full_lanes) * mask[None]).reshape(full_rows, full_lanes)

    def assemble(own, plane, slot=0):
        plane_ref[slot, 0:rows, 0:lanes] = own
        plane_ref[slot, rows : rows + HALO, 0:lanes] = ln_ref[0, plane]
        plane_ref[slot, rows + HALO : full_rows, 0:lanes] = lp_ref[0, plane]
        plane_ref[slot, :, lanes:full_lanes] = rt_ref[0, plane]
        return plane_ref[slot]

    w_east = assemble(wi_ref[0, 0], probes + 0)
    w_north = assemble(wi_ref[1, 0], probes + 1)
    t_east = assemble(te_ref[0, 0], probes + 2)
    t_north = assemble(te_ref[1, 0], probes + 3)
    for s in range(STEPS):
        east = 0.5 * (w_east + s * t_east)
        north = 0.5 * (w_north + s * t_north)
        coef_ref[s, 0] = k - east
        coef_ref[s, 1] = k + east
        coef_ref[s, 2] = k - north
        coef_ref[s, 3] = k + north
        coef_ref[s, 4] = shifted(k - east, -1, 0)
        coef_ref[s, 5] = shifted(k + east, 1, 0)
        coef_ref[s, 6] = shifted(k - north, -1, 1)
        coef_ref[s, 7] = shifted(k + north, 1, 1)
    coef_ref[STEPS, 0] = assemble(ob_ref[0], probes + 4)

    def probe_pair(i, carry):
        p = 2 * i
        fs = [assemble(pr_ref[p + j, 0], p + j, j) for j in range(2)]
        for s in range(STEPS):
            ce_m, ce_p, cn_m, cn_p = (coef_ref[s, c] for c in range(4))
            fs = [
                masked(
                    c0 * f
                    + ce_m * shifted(f, 1, 0)
                    + ce_p * shifted(f, -1, 0)
                    + cn_m * shifted(f, 1, 1)
                    + cn_p * shifted(f, -1, 1)
                )
                for f in fs
            ]
        weight = coef_ref[STEPS, 0]
        fs = [f * weight for f in fs]
        for s in reversed(range(STEPS)):
            aw, ae, as_, an = (coef_ref[s, c] for c in range(4, 8))
            fs = [
                masked(
                    c0 * f
                    + aw * shifted(f, -1, 0)
                    + ae * shifted(f, 1, 0)
                    + as_ * shifted(f, -1, 1)
                    + an * shifted(f, 1, 1)
                )
                for f in fs
            ]
        for j in range(2):
            o_ref[p + j, 0] = fs[j][:rows, :lanes]
        return carry

    lax.fori_loop(0, probes // 2, probe_pair, 0)
    for p in range(probes):
        for q in range(p, probes):
            prod = (o_ref[p, 0] * o_ref[q, 0]).reshape(rows // 8, 8, lanes)
            part = jnp.sum(jnp.sum(prod, axis=0), axis=0, keepdims=True)
            g_ref[0, pl.ds(p * probes + q, 1), :] = part
            if q != p:
                g_ref[0, pl.ds(q * probes + p, 1), :] = part


def transport(mask, probes, wind, wind_tend, obs_weight, lon_next, lon_prev, lat_block):
    n_probes, levels, rows, lanes = probes.shape
    planes = lon_next.shape[1]
    full_rows = rows + 2 * HALO
    full_lanes = 2 * lanes

    def level_block(lead):
        return pl.BlockSpec((lead, 1, rows, lanes), lambda l: (0, l, 0, 0))

    def halo_block(height):
        return pl.BlockSpec((1, planes, height, lanes), lambda l: (l, 0, 0, 0))

    return pl.pallas_call(
        transport_kernel,
        grid=(levels,),
        in_specs=[
            pl.BlockSpec((8, full_lanes), lambda l: (0, 0)),
            level_block(n_probes),
            level_block(2),
            level_block(2),
            pl.BlockSpec((1, rows, lanes), lambda l: (l, 0, 0)),
            halo_block(HALO),
            halo_block(HALO),
            halo_block(full_rows),
        ],
        out_specs=[
            level_block(n_probes),
            pl.BlockSpec((1, n_probes * n_probes, lanes), lambda l: (l, 0, 0)),
        ],
        out_shape=[
            jax.ShapeDtypeStruct((n_probes, levels, rows, lanes), jnp.float32),
            jax.ShapeDtypeStruct((levels, n_probes * n_probes, lanes), jnp.float32),
        ],
        scratch_shapes=[
            pltpu.VMEM((STEPS + 1, 8, full_rows, full_lanes), jnp.float32),
            pltpu.VMEM((2, full_rows, full_lanes), jnp.float32),
        ],
    )(mask, probes, wind, wind_tend, obs_weight, lon_next, lon_prev, lat_block)

def basis_kernel(inv_ref, scale_ref, z_ref, o_ref):
    probes = z_ref.shape[0]
    z = [z_ref[q, 0] for q in range(probes)]
    for p in range(probes):
        acc = inv_ref[p, 0] * z[0]
        for q in range(1, probes):
            acc = acc + inv_ref[p, q] * z[q]
        o_ref[p, 0] = acc * scale_ref[0, 0]


def basis(inverse, scale, field):
    probes, levels, rows, lanes = field.shape
    block = pl.BlockSpec((probes, 1, rows, lanes), lambda l: (0, l, 0, 0))
    return pl.pallas_call(
        basis_kernel,
        grid=(levels,),
        in_specs=[
            pl.BlockSpec(memory_space=pltpu.SMEM),
            pl.BlockSpec(memory_space=pltpu.SMEM),
            block,
        ],
        out_specs=block,
        out_shape=jax.ShapeDtypeStruct(field.shape, jnp.float32),
    )(inverse, scale, field)


def body(probes, wind, wind_tend, obs_weight):
    n_probes, levels, width_lon, width_lat = probes.shape

    def planes_of(part):
        return jnp.concatenate(
            (
                jnp.swapaxes(part(probes), 0, 1),
                jnp.swapaxes(part(wind), 0, 1),
                jnp.swapaxes(part(wind_tend), 0, 1),
                part(obs_weight[None])[0][:, None],
            ),
            axis=1,
        )

    heads = planes_of(lambda a: a[..., :HALO, :])
    tails = planes_of(lambda a: a[..., width_lon - HALO :, :])
    n_lon = lax.axis_size("lon")
    lon_next = lax.ppermute(heads, "lon", [((i + 1) % n_lon, i) for i in range(n_lon)])
    lon_prev = lax.ppermute(tails, "lon", [(i, (i + 1) % n_lon) for i in range(n_lon)])
    own_lo = planes_of(lambda a: a[..., :HALO])
    own_hi = planes_of(lambda a: a[..., width_lat - HALO :])
    edge_lo = jnp.concatenate((own_lo, lon_next[..., :HALO], lon_prev[..., :HALO]), axis=2)
    edge_hi = jnp.concatenate(
        (own_hi, lon_next[..., width_lat - HALO :], lon_prev[..., width_lat - HALO :]), axis=2
    )
    n_lat = lax.axis_size("lat")
    lat_next = lax.ppermute(jnp.swapaxes(edge_lo, 2, 3), "lat", [(j + 1, j) for j in range(n_lat - 1)])
    lat_prev = lax.ppermute(jnp.swapaxes(edge_hi, 2, 3), "lat", [(j, j + 1) for j in range(n_lat - 1)])
    gap = jnp.zeros(edge_lo.shape[:3] + (width_lat - 2 * HALO,), jnp.float32)
    lat_block = jnp.concatenate(
        (jnp.swapaxes(lat_next, 2, 3), gap, jnp.swapaxes(lat_prev, 2, 3)), axis=3
    )
    lanes = 2 * width_lat
    lane = lax.broadcasted_iota(jnp.int32, (8, lanes), 1)
    start = lax.axis_index("lat") * width_lat
    cell = jnp.where(lane < width_lat + HALO, start + lane, start + lane - lanes)
    inside = ((lane < width_lat + HALO) | (lane >= lanes - HALO)) & (cell >= 0)
    inside = inside & (cell < width_lat * n_lat)
    mask = inside.astype(jnp.float32)

    field, partial = transport(
        mask, probes, wind, wind_tend, obs_weight, lon_next, lon_prev, lat_block
    )

    gram = jnp.sum(partial, axis=(0, 2)).reshape(n_probes, n_probes)
    gram = all_sum(gram, ("lon", "lat"))
    lower = jnp.linalg.cholesky(gram)
    upper = lower.T
    cells = field.shape[1] * width_lon * width_lat * lax.axis_size("lat") * lax.axis_size("lon")
    scale = jnp.sqrt(jnp.float32(cells))
    result = basis(lower_inverse(lower), scale.reshape(1, 1), field)
    return (result, upper / scale)


def solution(mesh):
    placed = (
        P(None, None, "lon", "lat"),
        P(None, None, "lon", "lat"),
        P(None, None, "lon", "lat"),
        P(None, "lon", "lat"),
    )
    return jax.shard_map(
        body,
        mesh=mesh,
        in_specs=placed,
        out_specs=(P(None, None, "lon", "lat"), P()),
        check_vma=False,
    )
```

```python
import jax
import jax.numpy as jnp
from jax import lax
from jax.experimental import pallas as pl
from jax.experimental.pallas import tpu as pltpu
from jax.sharding import PartitionSpec as P

STEPS = 4
HALO = 2 * STEPS
GROUP = 4

diffuse = 0.24


def lower_inverse(lower):
    eye = jnp.eye(lower.shape[0], dtype=lower.dtype)
    return lax.linalg.triangular_solve(lower, eye, left_side=True, lower=True)


def all_sum(value, axes):
    for axis in axes:
        count = lax.axis_size(axis)
        if count & (count - 1):
            value = lax.psum(value, axis)
            continue
        stride = 1
        while stride < count:
            value = value + lax.ppermute(value, axis, [(i, i ^ stride) for i in range(count)])
            stride *= 2
    return value


def shifted(x, offset, axis):
    n = x.shape[axis]
    return pltpu.roll(x, (-offset) % n, axis)


def transport_kernel(
    mask_ref, pr_ref, wi_ref, te_ref, ob_ref, ln_ref, lp_ref, rt_ref, o_ref, g_ref, coef_ref, plane_ref
):
    k = diffuse
    c0 = 1.0 - 4.0 * diffuse
    probes = o_ref.shape[0]
    rows = o_ref.shape[2]
    lanes = o_ref.shape[3]
    full_rows, full_lanes = plane_ref.shape[1:]
    mask = mask_ref[...]

    def masked(f):
        return (f.reshape(full_rows // 8, 8, full_lanes) * mask[None]).reshape(full_rows, full_lanes)

    def assemble(own, plane, slot=0):
        plane_ref[slot, 0:rows, 0:lanes] = own
        plane_ref[slot, rows : rows + HALO, 0:lanes] = ln_ref[0, plane]
        plane_ref[slot, rows + HALO : full_rows, 0:lanes] = lp_ref[0, plane]
        plane_ref[slot, :, lanes:full_lanes] = rt_ref[0, plane]
        return plane_ref[slot]

    w_east = assemble(wi_ref[0, 0], probes + 0)
    w_north = assemble(wi_ref[1, 0], probes + 1)
    t_east = assemble(te_ref[0, 0], probes + 2)
    t_north = assemble(te_ref[1, 0], probes + 3)
    for s in range(STEPS):
        east = 0.5 * (w_east + s * t_east)
        north = 0.5 * (w_north + s * t_north)
        coef_ref[s, 0] = k - east
        coef_ref[s, 1] = k + east
        coef_ref[s, 2] = k - north
        coef_ref[s, 3] = k + north
        coef_ref[s, 4] = shifted(k - east, -1, 0)
        coef_ref[s, 5] = shifted(k + east, 1, 0)
        coef_ref[s, 6] = shifted(k - north, -1, 1)
        coef_ref[s, 7] = shifted(k + north, 1, 1)
    coef_ref[STEPS, 0] = assemble(ob_ref[0], probes + 4)

    def probe_pair(i, carry):
        p = GROUP * i
        fs = [assemble(pr_ref[p + j, 0], p + j, j) for j in range(GROUP)]
        for s in range(STEPS):
            ce_m, ce_p, cn_m, cn_p = (coef_ref[s, c] for c in range(4))
            fs = [
                masked(
                    c0 * f
                    + ce_m * shifted(f, 1, 0)
                    + ce_p * shifted(f, -1, 0)
                    + cn_m * shifted(f, 1, 1)
                    + cn_p * shifted(f, -1, 1)
                )
                for f in fs
            ]
        weight = coef_ref[STEPS, 0]
        fs = [f * weight for f in fs]
        for s in reversed(range(STEPS)):
            aw, ae, as_, an = (coef_ref[s, c] for c in range(4, 8))
            fs = [
                masked(
                    c0 * f
                    + aw * shifted(f, -1, 0)
                    + ae * shifted(f, 1, 0)
                    + as_ * shifted(f, -1, 1)
                    + an * shifted(f, 1, 1)
                )
                for f in fs
            ]
        for j in range(GROUP):
            o_ref[p + j, 0] = fs[j][:rows, :lanes]
        return carry

    lax.fori_loop(0, probes // GROUP, probe_pair, 0)
    for p in range(probes):
        for q in range(p, probes):
            prod = (o_ref[p, 0] * o_ref[q, 0]).reshape(rows // 8, 8, lanes)
            part = jnp.sum(jnp.sum(prod, axis=0), axis=0, keepdims=True)
            g_ref[0, pl.ds(p * probes + q, 1), :] = part
            if q != p:
                g_ref[0, pl.ds(q * probes + p, 1), :] = part


def transport(mask, probes, wind, wind_tend, obs_weight, lon_next, lon_prev, lat_block):
    n_probes, levels, rows, lanes = probes.shape
    planes = lon_next.shape[1]
    full_rows = rows + 2 * HALO
    full_lanes = 2 * lanes

    def level_block(lead):
        return pl.BlockSpec((lead, 1, rows, lanes), lambda l: (0, l, 0, 0))

    def halo_block(height):
        return pl.BlockSpec((1, planes, height, lanes), lambda l: (l, 0, 0, 0))

    return pl.pallas_call(
        transport_kernel,
        grid=(levels,),
        in_specs=[
            pl.BlockSpec((8, full_lanes), lambda l: (0, 0)),
            level_block(n_probes),
            level_block(2),
            level_block(2),
            pl.BlockSpec((1, rows, lanes), lambda l: (l, 0, 0)),
            halo_block(HALO),
            halo_block(HALO),
            halo_block(full_rows),
        ],
        out_specs=[
            level_block(n_probes),
            pl.BlockSpec((1, n_probes * n_probes, lanes), lambda l: (l, 0, 0)),
        ],
        out_shape=[
            jax.ShapeDtypeStruct((n_probes, levels, rows, lanes), jnp.float32),
            jax.ShapeDtypeStruct((levels, n_probes * n_probes, lanes), jnp.float32),
        ],
        scratch_shapes=[
            pltpu.VMEM((STEPS + 1, 8, full_rows, full_lanes), jnp.float32),
            pltpu.VMEM((GROUP, full_rows, full_lanes), jnp.float32),
        ],
    )(mask, probes, wind, wind_tend, obs_weight, lon_next, lon_prev, lat_block)

def basis_kernel(inv_ref, scale_ref, z_ref, o_ref):
    probes = z_ref.shape[0]
    z = [z_ref[q, 0] for q in range(probes)]
    for p in range(probes):
        acc = inv_ref[p, 0] * z[0]
        for q in range(1, probes):
            acc = acc + inv_ref[p, q] * z[q]
        o_ref[p, 0] = acc * scale_ref[0, 0]


def basis(inverse, scale, field):
    probes, levels, rows, lanes = field.shape
    block = pl.BlockSpec((probes, 1, rows, lanes), lambda l: (0, l, 0, 0))
    return pl.pallas_call(
        basis_kernel,
        grid=(levels,),
        in_specs=[
            pl.BlockSpec(memory_space=pltpu.SMEM),
            pl.BlockSpec(memory_space=pltpu.SMEM),
            block,
        ],
        out_specs=block,
        out_shape=jax.ShapeDtypeStruct(field.shape, jnp.float32),
    )(inverse, scale, field)


def body(probes, wind, wind_tend, obs_weight):
    n_probes, levels, width_lon, width_lat = probes.shape

    def planes_of(part):
        return jnp.concatenate(
            (
                jnp.swapaxes(part(probes), 0, 1),
                jnp.swapaxes(part(wind), 0, 1),
                jnp.swapaxes(part(wind_tend), 0, 1),
                part(obs_weight[None])[0][:, None],
            ),
            axis=1,
        )

    heads = planes_of(lambda a: a[..., :HALO, :])
    tails = planes_of(lambda a: a[..., width_lon - HALO :, :])
    n_lon = lax.axis_size("lon")
    lon_next = lax.ppermute(heads, "lon", [((i + 1) % n_lon, i) for i in range(n_lon)])
    lon_prev = lax.ppermute(tails, "lon", [(i, (i + 1) % n_lon) for i in range(n_lon)])
    own_lo = planes_of(lambda a: a[..., :HALO])
    own_hi = planes_of(lambda a: a[..., width_lat - HALO :])
    edge_lo = jnp.concatenate((own_lo, lon_next[..., :HALO], lon_prev[..., :HALO]), axis=2)
    edge_hi = jnp.concatenate(
        (own_hi, lon_next[..., width_lat - HALO :], lon_prev[..., width_lat - HALO :]), axis=2
    )
    n_lat = lax.axis_size("lat")
    lat_next = lax.ppermute(jnp.swapaxes(edge_lo, 2, 3), "lat", [(j + 1, j) for j in range(n_lat - 1)])
    lat_prev = lax.ppermute(jnp.swapaxes(edge_hi, 2, 3), "lat", [(j, j + 1) for j in range(n_lat - 1)])
    gap = jnp.zeros(edge_lo.shape[:3] + (width_lat - 2 * HALO,), jnp.float32)
    lat_block = jnp.concatenate(
        (jnp.swapaxes(lat_next, 2, 3), gap, jnp.swapaxes(lat_prev, 2, 3)), axis=3
    )
    lanes = 2 * width_lat
    lane = lax.broadcasted_iota(jnp.int32, (8, lanes), 1)
    start = lax.axis_index("lat") * width_lat
    cell = jnp.where(lane < width_lat + HALO, start + lane, start + lane - lanes)
    inside = ((lane < width_lat + HALO) | (lane >= lanes - HALO)) & (cell >= 0)
    inside = inside & (cell < width_lat * n_lat)
    mask = inside.astype(jnp.float32)

    field, partial = transport(
        mask, probes, wind, wind_tend, obs_weight, lon_next, lon_prev, lat_block
    )

    gram = jnp.sum(partial, axis=(0, 2)).reshape(n_probes, n_probes)
    gram = all_sum(gram, ("lon", "lat"))
    lower = jnp.linalg.cholesky(gram)
    upper = lower.T
    cells = field.shape[1] * width_lon * width_lat * lax.axis_size("lat") * lax.axis_size("lon")
    scale = jnp.sqrt(jnp.float32(cells))
    result = basis(lower_inverse(lower), scale.reshape(1, 1), field)
    return (result, upper / scale)


def solution(mesh):
    placed = (
        P(None, None, "lon", "lat"),
        P(None, None, "lon", "lat"),
        P(None, None, "lon", "lat"),
        P(None, "lon", "lat"),
    )
    return jax.shard_map(
        body,
        mesh=mesh,
        in_specs=placed,
        out_specs=(P(None, None, "lon", "lat"), P()),
        check_vma=False,
    )
```

```python
import jax
import jax.numpy as jnp
from jax import lax
from jax.experimental import pallas as pl
from jax.experimental.pallas import tpu as pltpu
from jax.sharding import PartitionSpec as P

STEPS = 4
HALO = 2 * STEPS
GROUP = 4

diffuse = 0.24


def lower_inverse(lower):
    eye = jnp.eye(lower.shape[0], dtype=lower.dtype)
    return lax.linalg.triangular_solve(lower, eye, left_side=True, lower=True)


def all_sum(value, axes):
    for axis in axes:
        count = lax.axis_size(axis)
        if count & (count - 1):
            value = lax.psum(value, axis)
            continue
        stride = 1
        while stride < count:
            value = value + lax.ppermute(value, axis, [(i, i ^ stride) for i in range(count)])
            stride *= 2
    return value


def shifted(x, offset, axis):
    n = x.shape[axis]
    return pltpu.roll(x, (-offset) % n, axis)


def transport_kernel(
    mask_ref, pr_ref, wi_ref, te_ref, ob_ref, ln_ref, lp_ref, un_ref, up_ref, o_ref, g_ref, coef_ref, plane_ref
):
    k = diffuse
    c0 = 1.0 - 4.0 * diffuse
    probes = o_ref.shape[0]
    rows = o_ref.shape[2]
    lanes = o_ref.shape[3]
    full_rows, full_lanes = plane_ref.shape[1:]
    mask = mask_ref[...]

    def masked(f):
        return (f.reshape(full_rows // 8, 8, full_lanes) * mask[None]).reshape(full_rows, full_lanes)

    def assemble(own, plane, slot=0):
        plane_ref[slot, 0:rows, 0:lanes] = own
        plane_ref[slot, rows : rows + HALO, 0:lanes] = ln_ref[0, plane]
        plane_ref[slot, rows + HALO : full_rows, 0:lanes] = lp_ref[0, plane]
        gap = jnp.zeros((lanes - 2 * HALO, lanes), jnp.float32)
        halo = jnp.concatenate((un_ref[0, plane], gap, up_ref[0, plane]), axis=0)
        plane_ref[slot, :, lanes:full_lanes] = halo.T[:full_rows]
        return plane_ref[slot]

    w_east = assemble(wi_ref[0, 0], probes + 0)
    w_north = assemble(wi_ref[1, 0], probes + 1)
    t_east = assemble(te_ref[0, 0], probes + 2)
    t_north = assemble(te_ref[1, 0], probes + 3)
    for s in range(STEPS):
        east = 0.5 * (w_east + s * t_east)
        north = 0.5 * (w_north + s * t_north)
        coef_ref[s, 0] = k - east
        coef_ref[s, 1] = k + east
        coef_ref[s, 2] = k - north
        coef_ref[s, 3] = k + north
        coef_ref[s, 4] = shifted(k - east, -1, 0)
        coef_ref[s, 5] = shifted(k + east, 1, 0)
        coef_ref[s, 6] = shifted(k - north, -1, 1)
        coef_ref[s, 7] = shifted(k + north, 1, 1)
    coef_ref[STEPS, 0] = assemble(ob_ref[0], probes + 4)

    def probe_pair(i, carry):
        p = GROUP * i
        fs = [assemble(pr_ref[p + j, 0], p + j, j) for j in range(GROUP)]
        for s in range(STEPS):
            ce_m, ce_p, cn_m, cn_p = (coef_ref[s, c] for c in range(4))
            fs = [
                masked(
                    c0 * f
                    + ce_m * shifted(f, 1, 0)
                    + ce_p * shifted(f, -1, 0)
                    + cn_m * shifted(f, 1, 1)
                    + cn_p * shifted(f, -1, 1)
                )
                for f in fs
            ]
        weight = coef_ref[STEPS, 0]
        fs = [f * weight for f in fs]
        for s in reversed(range(STEPS)):
            aw, ae, as_, an = (coef_ref[s, c] for c in range(4, 8))
            fs = [
                masked(
                    c0 * f
                    + aw * shifted(f, -1, 0)
                    + ae * shifted(f, 1, 0)
                    + as_ * shifted(f, -1, 1)
                    + an * shifted(f, 1, 1)
                )
                for f in fs
            ]
        for j in range(GROUP):
            o_ref[p + j, 0] = fs[j][:rows, :lanes]
        return carry

    lax.fori_loop(0, probes // GROUP, probe_pair, 0)
    for p in range(probes):
        for q in range(p, probes):
            prod = (o_ref[p, 0] * o_ref[q, 0]).reshape(rows // 8, 8, lanes)
            part = jnp.sum(jnp.sum(prod, axis=0), axis=0, keepdims=True)
            g_ref[0, pl.ds(p * probes + q, 1), :] = part
            if q != p:
                g_ref[0, pl.ds(q * probes + p, 1), :] = part


def transport(mask, probes, wind, wind_tend, obs_weight, lon_next, lon_prev, lat_next, lat_prev):
    n_probes, levels, rows, lanes = probes.shape
    planes = lon_next.shape[1]
    full_rows = rows + 2 * HALO
    full_lanes = 2 * lanes

    def level_block(lead):
        return pl.BlockSpec((lead, 1, rows, lanes), lambda l: (0, l, 0, 0))

    def halo_block(height):
        return pl.BlockSpec((1, planes, height, lanes), lambda l: (l, 0, 0, 0))

    return pl.pallas_call(
        transport_kernel,
        grid=(levels,),
        in_specs=[
            pl.BlockSpec((8, full_lanes), lambda l: (0, 0)),
            level_block(n_probes),
            level_block(2),
            level_block(2),
            pl.BlockSpec((1, rows, lanes), lambda l: (l, 0, 0)),
            halo_block(HALO),
            halo_block(HALO),
            halo_block(HALO),
            halo_block(HALO),
        ],
        out_specs=[
            level_block(n_probes),
            pl.BlockSpec((1, n_probes * n_probes, lanes), lambda l: (l, 0, 0)),
        ],
        out_shape=[
            jax.ShapeDtypeStruct((n_probes, levels, rows, lanes), jnp.float32),
            jax.ShapeDtypeStruct((levels, n_probes * n_probes, lanes), jnp.float32),
        ],
        scratch_shapes=[
            pltpu.VMEM((STEPS + 1, 8, full_rows, full_lanes), jnp.float32),
            pltpu.VMEM((GROUP, full_rows, full_lanes), jnp.float32),
        ],
    )(mask, probes, wind, wind_tend, obs_weight, lon_next, lon_prev, lat_next, lat_prev)

def basis_kernel(inv_ref, scale_ref, z_ref, o_ref):
    probes = z_ref.shape[0]
    scale = scale_ref[0, 0]

    def chunk(c, carry):
        rows = pl.ds(c * 8, 8)
        z = [z_ref[q, 0, rows, :] for q in range(probes)]
        for p in range(probes):
            acc = inv_ref[p, 0] * z[0]
            for q in range(1, probes):
                acc = acc + inv_ref[p, q] * z[q]
            o_ref[p, 0, rows, :] = acc * scale
        return carry

    lax.fori_loop(0, z_ref.shape[2] // 8, chunk, 0)


def basis(inverse, scale, field):
    probes, levels, rows, lanes = field.shape
    block = pl.BlockSpec((probes, 1, rows, lanes), lambda l: (0, l, 0, 0))
    return pl.pallas_call(
        basis_kernel,
        grid=(levels,),
        in_specs=[
            pl.BlockSpec(memory_space=pltpu.SMEM),
            pl.BlockSpec(memory_space=pltpu.SMEM),
            block,
        ],
        out_specs=block,
        out_shape=jax.ShapeDtypeStruct(field.shape, jnp.float32),
    )(inverse, scale, field)


def body(probes, wind, wind_tend, obs_weight):
    n_probes, levels, width_lon, width_lat = probes.shape

    def planes_of(part):
        return jnp.concatenate(
            (
                jnp.swapaxes(part(probes), 0, 1),
                jnp.swapaxes(part(wind), 0, 1),
                jnp.swapaxes(part(wind_tend), 0, 1),
                part(obs_weight[None])[0][:, None],
            ),
            axis=1,
        )

    heads = planes_of(lambda a: a[..., :HALO, :])
    tails = planes_of(lambda a: a[..., width_lon - HALO :, :])
    n_lon = lax.axis_size("lon")
    lon_next = lax.ppermute(heads, "lon", [((i + 1) % n_lon, i) for i in range(n_lon)])
    lon_prev = lax.ppermute(tails, "lon", [(i, (i + 1) % n_lon) for i in range(n_lon)])
    own_lo = planes_of(lambda a: a[..., :HALO])
    own_hi = planes_of(lambda a: a[..., width_lat - HALO :])
    fill = jnp.zeros(own_lo.shape[:2] + (width_lat - width_lon - 2 * HALO, HALO), jnp.float32)
    edge_lo = jnp.concatenate((own_lo, lon_next[..., :HALO], lon_prev[..., :HALO], fill), axis=2)
    edge_hi = jnp.concatenate(
        (own_hi, lon_next[..., width_lat - HALO :], lon_prev[..., width_lat - HALO :], fill), axis=2
    )
    n_lat = lax.axis_size("lat")
    lat_next = lax.ppermute(jnp.swapaxes(edge_lo, 2, 3), "lat", [(j + 1, j) for j in range(n_lat - 1)])
    lat_prev = lax.ppermute(jnp.swapaxes(edge_hi, 2, 3), "lat", [(j, j + 1) for j in range(n_lat - 1)])
    lanes = 2 * width_lat
    lane = lax.broadcasted_iota(jnp.int32, (8, lanes), 1)
    start = lax.axis_index("lat") * width_lat
    cell = jnp.where(lane < width_lat + HALO, start + lane, start + lane - lanes)
    inside = ((lane < width_lat + HALO) | (lane >= lanes - HALO)) & (cell >= 0)
    inside = inside & (cell < width_lat * n_lat)
    mask = inside.astype(jnp.float32)

    field, partial = transport(
        mask, probes, wind, wind_tend, obs_weight, lon_next, lon_prev, lat_next, lat_prev
    )

    gram = jnp.sum(partial, axis=(0, 2)).reshape(n_probes, n_probes)
    gram = all_sum(gram, ("lon", "lat"))
    lower = jnp.linalg.cholesky(gram)
    upper = lower.T
    cells = field.shape[1] * width_lon * width_lat * lax.axis_size("lat") * lax.axis_size("lon")
    scale = jnp.sqrt(jnp.float32(cells))
    result = basis(lower_inverse(lower), scale.reshape(1, 1), field)
    return (result, upper / scale)


def solution(mesh):
    placed = (
        P(None, None, "lon", "lat"),
        P(None, None, "lon", "lat"),
        P(None, None, "lon", "lat"),
        P(None, "lon", "lat"),
    )
    return jax.shard_map(
        body,
        mesh=mesh,
        in_specs=placed,
        out_specs=(P(None, None, "lon", "lat"), P()),
        check_vma=False,
    )
```

```python
import jax
import jax.numpy as jnp
from jax import lax
from jax.experimental import pallas as pl
from jax.experimental.pallas import tpu as pltpu
from jax.sharding import PartitionSpec as P

STEPS = 4
HALO = 2 * STEPS
GROUP = 8

diffuse = 0.24


def lower_inverse(lower):
    eye = jnp.eye(lower.shape[0], dtype=lower.dtype)
    return lax.linalg.triangular_solve(lower, eye, left_side=True, lower=True)


def all_sum(value, axes):
    for axis in axes:
        count = lax.axis_size(axis)
        if count & (count - 1):
            value = lax.psum(value, axis)
            continue
        stride = 1
        while stride < count:
            value = value + lax.ppermute(value, axis, [(i, i ^ stride) for i in range(count)])
            stride *= 2
    return value


def shifted(x, offset, axis):
    n = x.shape[axis]
    return pltpu.roll(x, (-offset) % n, axis)


def transport_kernel(
    mask_ref, pr_ref, wi_ref, te_ref, ob_ref, ln_ref, lp_ref, un_ref, up_ref, o_ref, g_ref, coef_ref, plane_ref
):
    k = diffuse
    c0 = 1.0 - 4.0 * diffuse
    probes = o_ref.shape[0]
    rows = o_ref.shape[2]
    lanes = o_ref.shape[3]
    full_rows, full_lanes = plane_ref.shape[1:]
    mask = mask_ref[...]

    def masked(f):
        return (f.reshape(full_rows // 8, 8, full_lanes) * mask[None]).reshape(full_rows, full_lanes)

    def assemble(own, plane, slot=0):
        plane_ref[slot, 0:rows, 0:lanes] = own
        plane_ref[slot, rows : rows + HALO, 0:lanes] = ln_ref[0, plane]
        plane_ref[slot, rows + HALO : full_rows, 0:lanes] = lp_ref[0, plane]
        gap = jnp.zeros((lanes - 2 * HALO, lanes), jnp.float32)
        halo = jnp.concatenate((un_ref[0, plane], gap, up_ref[0, plane]), axis=0)
        plane_ref[slot, :, lanes:full_lanes] = halo.T[:full_rows]
        return plane_ref[slot]

    w_east = assemble(wi_ref[0, 0], probes + 0)
    w_north = assemble(wi_ref[1, 0], probes + 1)
    t_east = assemble(te_ref[0, 0], probes + 2)
    t_north = assemble(te_ref[1, 0], probes + 3)
    for s in range(STEPS):
        east = 0.5 * (w_east + s * t_east)
        north = 0.5 * (w_north + s * t_north)
        coef_ref[s, 0] = k - east
        coef_ref[s, 1] = k + east
        coef_ref[s, 2] = k - north
        coef_ref[s, 3] = k + north
        coef_ref[s, 4] = shifted(k - east, -1, 0)
        coef_ref[s, 5] = shifted(k + east, 1, 0)
        coef_ref[s, 6] = shifted(k - north, -1, 1)
        coef_ref[s, 7] = shifted(k + north, 1, 1)
    coef_ref[STEPS, 0] = assemble(ob_ref[0], probes + 4)

    def probe_pair(i, carry):
        p = GROUP * i
        fs = [assemble(pr_ref[p + j, 0], p + j, j) for j in range(GROUP)]
        for s in range(STEPS):
            ce_m, ce_p, cn_m, cn_p = (coef_ref[s, c] for c in range(4))
            fs = [
                masked(
                    c0 * f
                    + ce_m * shifted(f, 1, 0)
                    + ce_p * shifted(f, -1, 0)
                    + cn_m * shifted(f, 1, 1)
                    + cn_p * shifted(f, -1, 1)
                )
                for f in fs
            ]
        weight = coef_ref[STEPS, 0]
        fs = [f * weight for f in fs]
        for s in reversed(range(STEPS)):
            aw, ae, as_, an = (coef_ref[s, c] for c in range(4, 8))
            fs = [
                masked(
                    c0 * f
                    + aw * shifted(f, -1, 0)
                    + ae * shifted(f, 1, 0)
                    + as_ * shifted(f, -1, 1)
                    + an * shifted(f, 1, 1)
                )
                for f in fs
            ]
        for j in range(GROUP):
            o_ref[p + j, 0] = fs[j][:rows, :lanes]
        return carry

    lax.fori_loop(0, probes // GROUP, probe_pair, 0)
    for p in range(probes):
        for q in range(p, probes):
            prod = (o_ref[p, 0] * o_ref[q, 0]).reshape(rows // 8, 8, lanes)
            part = jnp.sum(jnp.sum(prod, axis=0), axis=0, keepdims=True)
            g_ref[0, pl.ds(p * probes + q, 1), :] = part
            if q != p:
                g_ref[0, pl.ds(q * probes + p, 1), :] = part


def transport(mask, probes, wind, wind_tend, obs_weight, lon_next, lon_prev, lat_next, lat_prev):
    n_probes, levels, rows, lanes = probes.shape
    planes = lon_next.shape[1]
    full_rows = rows + 2 * HALO
    full_lanes = 2 * lanes

    def level_block(lead):
        return pl.BlockSpec((lead, 1, rows, lanes), lambda l: (0, l, 0, 0))

    def halo_block(height):
        return pl.BlockSpec((1, planes, height, lanes), lambda l: (l, 0, 0, 0))

    return pl.pallas_call(
        transport_kernel,
        grid=(levels,),
        in_specs=[
            pl.BlockSpec((8, full_lanes), lambda l: (0, 0)),
            level_block(n_probes),
            level_block(2),
            level_block(2),
            pl.BlockSpec((1, rows, lanes), lambda l: (l, 0, 0)),
            halo_block(HALO),
            halo_block(HALO),
            halo_block(HALO),
            halo_block(HALO),
        ],
        out_specs=[
            level_block(n_probes),
            pl.BlockSpec((1, n_probes * n_probes, lanes), lambda l: (l, 0, 0)),
        ],
        out_shape=[
            jax.ShapeDtypeStruct((n_probes, levels, rows, lanes), jnp.float32),
            jax.ShapeDtypeStruct((levels, n_probes * n_probes, lanes), jnp.float32),
        ],
        scratch_shapes=[
            pltpu.VMEM((STEPS + 1, 8, full_rows, full_lanes), jnp.float32),
            pltpu.VMEM((GROUP, full_rows, full_lanes), jnp.float32),
        ],
    )(mask, probes, wind, wind_tend, obs_weight, lon_next, lon_prev, lat_next, lat_prev)

def basis_kernel(inv_ref, scale_ref, z_ref, o_ref):
    probes = z_ref.shape[0]
    scale = scale_ref[0, 0]

    def chunk(c, carry):
        rows = pl.ds(c * 8, 8)
        z = [z_ref[q, 0, rows, :] for q in range(probes)]
        for p in range(probes):
            acc = inv_ref[p, 0] * z[0]
            for q in range(1, probes):
                acc = acc + inv_ref[p, q] * z[q]
            o_ref[p, 0, rows, :] = acc * scale
        return carry

    lax.fori_loop(0, z_ref.shape[2] // 8, chunk, 0)


def basis(inverse, scale, field):
    probes, levels, rows, lanes = field.shape
    block = pl.BlockSpec((probes, 1, rows, lanes), lambda l: (0, l, 0, 0))
    return pl.pallas_call(
        basis_kernel,
        grid=(levels,),
        in_specs=[
            pl.BlockSpec(memory_space=pltpu.SMEM),
            pl.BlockSpec(memory_space=pltpu.SMEM),
            block,
        ],
        out_specs=block,
        out_shape=jax.ShapeDtypeStruct(field.shape, jnp.float32),
    )(inverse, scale, field)


def body(probes, wind, wind_tend, obs_weight):
    n_probes, levels, width_lon, width_lat = probes.shape

    def planes_of(part):
        return jnp.concatenate(
            (
                jnp.swapaxes(part(probes), 0, 1),
                jnp.swapaxes(part(wind), 0, 1),
                jnp.swapaxes(part(wind_tend), 0, 1),
                part(obs_weight[None])[0][:, None],
            ),
            axis=1,
        )

    heads = planes_of(lambda a: a[..., :HALO, :])
    tails = planes_of(lambda a: a[..., width_lon - HALO :, :])
    n_lon = lax.axis_size("lon")
    lon_next = lax.ppermute(heads, "lon", [((i + 1) % n_lon, i) for i in range(n_lon)])
    lon_prev = lax.ppermute(tails, "lon", [(i, (i + 1) % n_lon) for i in range(n_lon)])
    own_lo = planes_of(lambda a: a[..., :HALO])
    own_hi = planes_of(lambda a: a[..., width_lat - HALO :])
    fill = jnp.zeros(own_lo.shape[:2] + (width_lat - width_lon - 2 * HALO, HALO), jnp.float32)
    edge_lo = jnp.concatenate((own_lo, lon_next[..., :HALO], lon_prev[..., :HALO], fill), axis=2)
    edge_hi = jnp.concatenate(
        (own_hi, lon_next[..., width_lat - HALO :], lon_prev[..., width_lat - HALO :], fill), axis=2
    )
    n_lat = lax.axis_size("lat")
    lat_next = lax.ppermute(jnp.swapaxes(edge_lo, 2, 3), "lat", [(j + 1, j) for j in range(n_lat - 1)])
    lat_prev = lax.ppermute(jnp.swapaxes(edge_hi, 2, 3), "lat", [(j, j + 1) for j in range(n_lat - 1)])
    lanes = 2 * width_lat
    lane = lax.broadcasted_iota(jnp.int32, (8, lanes), 1)
    start = lax.axis_index("lat") * width_lat
    cell = jnp.where(lane < width_lat + HALO, start + lane, start + lane - lanes)
    inside = ((lane < width_lat + HALO) | (lane >= lanes - HALO)) & (cell >= 0)
    inside = inside & (cell < width_lat * n_lat)
    mask = inside.astype(jnp.float32)

    field, partial = transport(
        mask, probes, wind, wind_tend, obs_weight, lon_next, lon_prev, lat_next, lat_prev
    )

    gram = jnp.sum(partial, axis=(0, 2)).reshape(n_probes, n_probes)
    gram = all_sum(gram, ("lon", "lat"))
    lower = jnp.linalg.cholesky(gram)
    upper = lower.T
    cells = field.shape[1] * width_lon * width_lat * lax.axis_size("lat") * lax.axis_size("lon")
    scale = jnp.sqrt(jnp.float32(cells))
    result = basis(lower_inverse(lower), scale.reshape(1, 1), field)
    return (result, upper / scale)


def solution(mesh):
    placed = (
        P(None, None, "lon", "lat"),
        P(None, None, "lon", "lat"),
        P(None, None, "lon", "lat"),
        P(None, "lon", "lat"),
    )
    return jax.shard_map(
        body,
        mesh=mesh,
        in_specs=placed,
        out_specs=(P(None, None, "lon", "lat"), P()),
        check_vma=False,
    )
```

```python
import jax
import jax.numpy as jnp
from jax import lax
from jax.experimental import pallas as pl
from jax.experimental.pallas import tpu as pltpu
from jax.sharding import PartitionSpec as P

STEPS = 4
HALO = 2 * STEPS
GROUP = 8

diffuse = 0.24


def lower_inverse(lower):
    eye = jnp.eye(lower.shape[0], dtype=lower.dtype)
    return lax.linalg.triangular_solve(lower, eye, left_side=True, lower=True)


def all_sum(value, axes):
    for axis in axes:
        count = lax.axis_size(axis)
        if count & (count - 1):
            value = lax.psum(value, axis)
            continue
        stride = 1
        while stride < count:
            value = value + lax.ppermute(value, axis, [(i, i ^ stride) for i in range(count)])
            stride *= 2
    return value


def shifted(x, offset, axis):
    n = x.shape[axis]
    return pltpu.roll(x, (-offset) % n, axis)


def transport_kernel(
    mask_ref, pr_ref, wi_ref, te_ref, ob_ref, ln_ref, lp_ref, un_ref, up_ref, o_ref, g_ref, coef_ref, plane_ref
):
    k = diffuse
    c0 = 1.0 - 4.0 * diffuse
    probes = o_ref.shape[0]
    rows = o_ref.shape[2]
    lanes = o_ref.shape[3]
    full_rows, full_lanes = plane_ref.shape[1:]
    mask = mask_ref[...]

    def masked(f):
        return (f.reshape(full_rows // 8, 8, full_lanes) * mask[None]).reshape(full_rows, full_lanes)

    def assemble(own, plane, slot=0):
        plane_ref[slot, 0:rows, 0:lanes] = own
        plane_ref[slot, rows : rows + HALO, 0:lanes] = ln_ref[plane, 0]
        plane_ref[slot, rows + HALO : full_rows, 0:lanes] = lp_ref[plane, 0]
        gap = jnp.zeros((lanes - 2 * HALO, lanes), jnp.float32)
        halo = jnp.concatenate((un_ref[plane, 0], gap, up_ref[plane, 0]), axis=0)
        plane_ref[slot, :, lanes:full_lanes] = halo.T[:full_rows]
        return plane_ref[slot]

    w_east = assemble(wi_ref[0, 0], probes + 0)
    w_north = assemble(wi_ref[1, 0], probes + 1)
    t_east = assemble(te_ref[0, 0], probes + 2)
    t_north = assemble(te_ref[1, 0], probes + 3)
    for s in range(STEPS):
        east = 0.5 * (w_east + s * t_east)
        north = 0.5 * (w_north + s * t_north)
        coef_ref[s, 0] = k - east
        coef_ref[s, 1] = k + east
        coef_ref[s, 2] = k - north
        coef_ref[s, 3] = k + north
        coef_ref[s, 4] = shifted(k - east, -1, 0)
        coef_ref[s, 5] = shifted(k + east, 1, 0)
        coef_ref[s, 6] = shifted(k - north, -1, 1)
        coef_ref[s, 7] = shifted(k + north, 1, 1)
    coef_ref[STEPS, 0] = assemble(ob_ref[0], probes + 4)

    def probe_pair(i, carry):
        p = GROUP * i
        fs = [assemble(pr_ref[p + j, 0], p + j, j) for j in range(GROUP)]
        for s in range(STEPS):
            ce_m, ce_p, cn_m, cn_p = (coef_ref[s, c] for c in range(4))
            fs = [
                masked(
                    c0 * f
                    + ce_m * shifted(f, 1, 0)
                    + ce_p * shifted(f, -1, 0)
                    + cn_m * shifted(f, 1, 1)
                    + cn_p * shifted(f, -1, 1)
                )
                for f in fs
            ]
        weight = coef_ref[STEPS, 0]
        fs = [f * weight for f in fs]
        for s in reversed(range(STEPS)):
            aw, ae, as_, an = (coef_ref[s, c] for c in range(4, 8))
            fs = [
                masked(
                    c0 * f
                    + aw * shifted(f, -1, 0)
                    + ae * shifted(f, 1, 0)
                    + as_ * shifted(f, -1, 1)
                    + an * shifted(f, 1, 1)
                )
                for f in fs
            ]
        for j in range(GROUP):
            o_ref[p + j, 0] = fs[j][:rows, :lanes]
        return carry

    lax.fori_loop(0, probes // GROUP, probe_pair, 0)
    for p in range(probes):
        for q in range(p, probes):
            prod = (o_ref[p, 0] * o_ref[q, 0]).reshape(rows // 8, 8, lanes)
            part = jnp.sum(jnp.sum(prod, axis=0), axis=0, keepdims=True)
            g_ref[0, pl.ds(p * probes + q, 1), :] = part
            if q != p:
                g_ref[0, pl.ds(q * probes + p, 1), :] = part


def transport(mask, probes, wind, wind_tend, obs_weight, lon_next, lon_prev, lat_next, lat_prev):
    n_probes, levels, rows, lanes = probes.shape
    planes = lon_next.shape[0]
    full_rows = rows + 2 * HALO
    full_lanes = 2 * lanes

    def level_block(lead):
        return pl.BlockSpec((lead, 1, rows, lanes), lambda l: (0, l, 0, 0))

    def halo_block(height):
        return pl.BlockSpec((planes, 1, height, lanes), lambda l: (0, l, 0, 0))

    return pl.pallas_call(
        transport_kernel,
        grid=(levels,),
        in_specs=[
            pl.BlockSpec((8, full_lanes), lambda l: (0, 0)),
            level_block(n_probes),
            level_block(2),
            level_block(2),
            pl.BlockSpec((1, rows, lanes), lambda l: (l, 0, 0)),
            halo_block(HALO),
            halo_block(HALO),
            halo_block(HALO),
            halo_block(HALO),
        ],
        out_specs=[
            level_block(n_probes),
            pl.BlockSpec((1, n_probes * n_probes, lanes), lambda l: (l, 0, 0)),
        ],
        out_shape=[
            jax.ShapeDtypeStruct((n_probes, levels, rows, lanes), jnp.float32),
            jax.ShapeDtypeStruct((levels, n_probes * n_probes, lanes), jnp.float32),
        ],
        scratch_shapes=[
            pltpu.VMEM((STEPS + 1, 8, full_rows, full_lanes), jnp.float32),
            pltpu.VMEM((GROUP, full_rows, full_lanes), jnp.float32),
        ],
    )(mask, probes, wind, wind_tend, obs_weight, lon_next, lon_prev, lat_next, lat_prev)

def basis_kernel(inv_ref, scale_ref, z_ref, o_ref):
    probes = z_ref.shape[0]
    scale = scale_ref[0, 0]

    def chunk(c, carry):
        rows = pl.ds(c * 8, 8)
        z = [z_ref[q, 0, rows, :] for q in range(probes)]
        for p in range(probes):
            acc = inv_ref[p, 0] * z[0]
            for q in range(1, probes):
                acc = acc + inv_ref[p, q] * z[q]
            o_ref[p, 0, rows, :] = acc * scale
        return carry

    lax.fori_loop(0, z_ref.shape[2] // 8, chunk, 0)


def basis(inverse, scale, field):
    probes, levels, rows, lanes = field.shape
    block = pl.BlockSpec((probes, 1, rows, lanes), lambda l: (0, l, 0, 0))
    return pl.pallas_call(
        basis_kernel,
        grid=(levels,),
        in_specs=[
            pl.BlockSpec(memory_space=pltpu.SMEM),
            pl.BlockSpec(memory_space=pltpu.SMEM),
            block,
        ],
        out_specs=block,
        out_shape=jax.ShapeDtypeStruct(field.shape, jnp.float32),
    )(inverse, scale, field)


def body(probes, wind, wind_tend, obs_weight):
    n_probes, levels, width_lon, width_lat = probes.shape

    def planes_of(part):
        return jnp.concatenate(
            (part(probes), part(wind), part(wind_tend), part(obs_weight[None])), axis=0
        )

    heads = planes_of(lambda a: a[..., :HALO, :])
    tails = planes_of(lambda a: a[..., width_lon - HALO :, :])
    n_lon = lax.axis_size("lon")
    lon_next = lax.ppermute(heads, "lon", [((i + 1) % n_lon, i) for i in range(n_lon)])
    lon_prev = lax.ppermute(tails, "lon", [(i, (i + 1) % n_lon) for i in range(n_lon)])
    own_lo = planes_of(lambda a: a[..., :HALO])
    own_hi = planes_of(lambda a: a[..., width_lat - HALO :])
    fill = jnp.zeros(own_lo.shape[:2] + (width_lat - width_lon - 2 * HALO, HALO), jnp.float32)
    edge_lo = jnp.concatenate((own_lo, lon_next[..., :HALO], lon_prev[..., :HALO], fill), axis=2)
    edge_hi = jnp.concatenate(
        (own_hi, lon_next[..., width_lat - HALO :], lon_prev[..., width_lat - HALO :], fill), axis=2
    )
    n_lat = lax.axis_size("lat")
    lat_next = lax.ppermute(jnp.swapaxes(edge_lo, 2, 3), "lat", [(j + 1, j) for j in range(n_lat - 1)])
    lat_prev = lax.ppermute(jnp.swapaxes(edge_hi, 2, 3), "lat", [(j, j + 1) for j in range(n_lat - 1)])
    lanes = 2 * width_lat
    lane = lax.broadcasted_iota(jnp.int32, (8, lanes), 1)
    start = lax.axis_index("lat") * width_lat
    cell = jnp.where(lane < width_lat + HALO, start + lane, start + lane - lanes)
    inside = ((lane < width_lat + HALO) | (lane >= lanes - HALO)) & (cell >= 0)
    inside = inside & (cell < width_lat * n_lat)
    mask = inside.astype(jnp.float32)

    field, partial = transport(
        mask, probes, wind, wind_tend, obs_weight, lon_next, lon_prev, lat_next, lat_prev
    )

    gram = jnp.sum(partial, axis=(0, 2)).reshape(n_probes, n_probes)
    gram = all_sum(gram, ("lon", "lat"))
    lower = jnp.linalg.cholesky(gram)
    upper = lower.T
    cells = field.shape[1] * width_lon * width_lat * lax.axis_size("lat") * lax.axis_size("lon")
    scale = jnp.sqrt(jnp.float32(cells))
    result = basis(lower_inverse(lower), scale.reshape(1, 1), field)
    return (result, upper / scale)


def solution(mesh):
    placed = (
        P(None, None, "lon", "lat"),
        P(None, None, "lon", "lat"),
        P(None, None, "lon", "lat"),
        P(None, "lon", "lat"),
    )
    return jax.shard_map(
        body,
        mesh=mesh,
        in_specs=placed,
        out_specs=(P(None, None, "lon", "lat"), P()),
        check_vma=False,
    )
```

```python
import jax
import jax.numpy as jnp
from jax import lax
from jax.experimental import pallas as pl
from jax.experimental.pallas import tpu as pltpu
from jax.sharding import PartitionSpec as P

STEPS = 4
HALO = 2 * STEPS
GROUP = 8

diffuse = 0.24


def lower_inverse(lower):
    eye = jnp.eye(lower.shape[0], dtype=lower.dtype)
    return lax.linalg.triangular_solve(lower, eye, left_side=True, lower=True)


def all_sum(value, axes):
    for axis in axes:
        count = lax.axis_size(axis)
        if count & (count - 1):
            value = lax.psum(value, axis)
            continue
        stride = 1
        while stride < count:
            value = value + lax.ppermute(value, axis, [(i, i ^ stride) for i in range(count)])
            stride *= 2
    return value


def shifted(x, offset, axis):
    n = x.shape[axis]
    return pltpu.roll(x, (-offset) % n, axis)


def transport_kernel(
    mask_ref, pr_ref, wi_ref, te_ref, ob_ref, ln_ref, lp_ref, un_ref, up_ref, o_ref, g_ref, coef_ref, plane_ref
):
    k = diffuse
    c0 = 1.0 - 4.0 * diffuse
    probes = o_ref.shape[0]
    rows = o_ref.shape[2]
    lanes = o_ref.shape[3]
    full_rows, full_lanes = plane_ref.shape[1:]
    mask = mask_ref[...]

    def masked(f):
        return (f.reshape(full_rows // 8, 8, full_lanes) * mask[None]).reshape(full_rows, full_lanes)

    def assemble(own, plane, slot=0):
        plane_ref[slot, 0:rows, 0:lanes] = own
        plane_ref[slot, rows : rows + HALO, 0:lanes] = ln_ref[0, plane]
        plane_ref[slot, rows + HALO : full_rows, 0:lanes] = lp_ref[0, plane]
        gap = jnp.zeros((lanes - 2 * HALO, lanes), jnp.float32)
        halo = jnp.concatenate((un_ref[0, plane], gap, up_ref[0, plane]), axis=0)
        plane_ref[slot, :, lanes:full_lanes] = halo.T[:full_rows]
        return plane_ref[slot]

    w_east = assemble(wi_ref[0, 0], probes + 0)
    w_north = assemble(wi_ref[1, 0], probes + 1)
    t_east = assemble(te_ref[0, 0], probes + 2)
    t_north = assemble(te_ref[1, 0], probes + 3)
    for s in range(STEPS):
        east = 0.5 * (w_east + s * t_east)
        north = 0.5 * (w_north + s * t_north)
        coef_ref[s, 0] = k - east
        coef_ref[s, 1] = k + east
        coef_ref[s, 2] = k - north
        coef_ref[s, 3] = k + north
        coef_ref[s, 4] = shifted(k - east, -1, 0)
        coef_ref[s, 5] = shifted(k + east, 1, 0)
        coef_ref[s, 6] = shifted(k - north, -1, 1)
        coef_ref[s, 7] = shifted(k + north, 1, 1)
    coef_ref[STEPS, 0] = assemble(ob_ref[0], probes + 4)

    def probe_pair(i, carry):
        p = GROUP * i
        fs = [assemble(pr_ref[p + j, 0], p + j, j) for j in range(GROUP)]
        for s in range(STEPS):
            ce_m, ce_p, cn_m, cn_p = (coef_ref[s, c] for c in range(4))
            fs = [
                masked(
                    c0 * f
                    + ce_m * shifted(f, 1, 0)
                    + ce_p * shifted(f, -1, 0)
                    + cn_m * shifted(f, 1, 1)
                    + cn_p * shifted(f, -1, 1)
                )
                for f in fs
            ]
        weight = coef_ref[STEPS, 0]
        fs = [f * weight for f in fs]
        for s in reversed(range(STEPS)):
            aw, ae, as_, an = (coef_ref[s, c] for c in range(4, 8))
            fs = [
                masked(
                    c0 * f
                    + aw * shifted(f, -1, 0)
                    + ae * shifted(f, 1, 0)
                    + as_ * shifted(f, -1, 1)
                    + an * shifted(f, 1, 1)
                )
                for f in fs
            ]
        for j in range(GROUP):
            o_ref[p + j, 0] = fs[j][:rows, :lanes]
        return carry

    lax.fori_loop(0, probes // GROUP, probe_pair, 0)
    for p in range(probes):
        for q in range(p, probes):
            prod = (o_ref[p, 0] * o_ref[q, 0]).reshape(rows // 8, 8, lanes)
            part = jnp.sum(jnp.sum(prod, axis=0), axis=0, keepdims=True)
            g_ref[0, pl.ds(p * probes + q, 1), :] = part
            if q != p:
                g_ref[0, pl.ds(q * probes + p, 1), :] = part


def transport(mask, probes, wind, wind_tend, obs_weight, lon_next, lon_prev, lat_next, lat_prev):
    n_probes, levels, rows, lanes = probes.shape
    planes = lon_next.shape[1]
    full_rows = rows + 2 * HALO
    full_lanes = 2 * lanes

    def level_block(lead):
        return pl.BlockSpec((lead, 1, rows, lanes), lambda l: (0, l, 0, 0))

    def halo_block(height):
        return pl.BlockSpec((1, planes, height, lanes), lambda l: (l, 0, 0, 0))

    return pl.pallas_call(
        transport_kernel,
        grid=(levels,),
        in_specs=[
            pl.BlockSpec((8, full_lanes), lambda l: (0, 0)),
            level_block(n_probes),
            level_block(2),
            level_block(2),
            pl.BlockSpec((1, rows, lanes), lambda l: (l, 0, 0)),
            halo_block(HALO),
            halo_block(HALO),
            halo_block(HALO),
            halo_block(HALO),
        ],
        out_specs=[
            level_block(n_probes),
            pl.BlockSpec((1, n_probes * n_probes, lanes), lambda l: (l, 0, 0)),
        ],
        out_shape=[
            jax.ShapeDtypeStruct((n_probes, levels, rows, lanes), jnp.float32),
            jax.ShapeDtypeStruct((levels, n_probes * n_probes, lanes), jnp.float32),
        ],
        scratch_shapes=[
            pltpu.VMEM((STEPS + 1, 8, full_rows, full_lanes), jnp.float32),
            pltpu.VMEM((GROUP, full_rows, full_lanes), jnp.float32),
        ],
    )(mask, probes, wind, wind_tend, obs_weight, lon_next, lon_prev, lat_next, lat_prev)

def basis_kernel(inv_ref, scale_ref, z_ref, o_ref):
    probes = z_ref.shape[0]
    scale = scale_ref[0, 0]

    def chunk(c, carry):
        rows = pl.ds(c * 8, 8)
        z = [z_ref[q, 0, rows, :] for q in range(probes)]
        for p in range(probes):
            acc = inv_ref[p, 0] * z[0]
            for q in range(1, probes):
                acc = acc + inv_ref[p, q] * z[q]
            o_ref[p, 0, rows, :] = acc * scale
        return carry

    lax.fori_loop(0, z_ref.shape[2] // 8, chunk, 0)


def basis(inverse, scale, field):
    probes, levels, rows, lanes = field.shape
    block = pl.BlockSpec((probes, 1, rows, lanes), lambda l: (0, l, 0, 0))
    return pl.pallas_call(
        basis_kernel,
        grid=(levels,),
        in_specs=[
            pl.BlockSpec(memory_space=pltpu.SMEM),
            pl.BlockSpec(memory_space=pltpu.SMEM),
            block,
        ],
        out_specs=block,
        out_shape=jax.ShapeDtypeStruct(field.shape, jnp.float32),
    )(inverse, scale, field)


def body(probes, wind, wind_tend, obs_weight):
    n_probes, levels, width_lon, width_lat = probes.shape

    def planes_of(part):
        return jnp.concatenate(
            (
                jnp.swapaxes(part(probes), 0, 1),
                jnp.swapaxes(part(wind), 0, 1),
                jnp.swapaxes(part(wind_tend), 0, 1),
                part(obs_weight[None])[0][:, None],
            ),
            axis=1,
        )

    heads = planes_of(lambda a: a[..., :HALO, :])
    tails = planes_of(lambda a: a[..., width_lon - HALO :, :])
    n_lon = lax.axis_size("lon")
    lon_next = lax.ppermute(heads, "lon", [((i + 1) % n_lon, i) for i in range(n_lon)])
    lon_prev = lax.ppermute(tails, "lon", [(i, (i + 1) % n_lon) for i in range(n_lon)])
    own_lo = planes_of(lambda a: a[..., :HALO])
    own_hi = planes_of(lambda a: a[..., width_lat - HALO :])
    fill = jnp.zeros(own_lo.shape[:2] + (width_lat - width_lon - 2 * HALO, HALO), jnp.float32)
    edge_lo = jnp.concatenate((own_lo, lon_next[..., :HALO], lon_prev[..., :HALO], fill), axis=2)
    edge_hi = jnp.concatenate(
        (own_hi, lon_next[..., width_lat - HALO :], lon_prev[..., width_lat - HALO :], fill), axis=2
    )
    n_lat = lax.axis_size("lat")
    lat_next = lax.ppermute(jnp.swapaxes(edge_lo, 2, 3), "lat", [(j + 1, j) for j in range(n_lat - 1)])
    lat_prev = lax.ppermute(jnp.swapaxes(edge_hi, 2, 3), "lat", [(j, j + 1) for j in range(n_lat - 1)])
    lanes = 2 * width_lat
    lane = lax.broadcasted_iota(jnp.int32, (8, lanes), 1)
    start = lax.axis_index("lat") * width_lat
    cell = jnp.where(lane < width_lat + HALO, start + lane, start + lane - lanes)
    inside = ((lane < width_lat + HALO) | (lane >= lanes - HALO)) & (cell >= 0)
    inside = inside & (cell < width_lat * n_lat)
    mask = inside.astype(jnp.float32)

    field, partial = transport(
        mask, probes, wind, wind_tend, obs_weight, lon_next, lon_prev, lat_next, lat_prev
    )

    gram = jnp.sum(partial, axis=(0, 2)).reshape(n_probes, n_probes)
    gram = all_sum(gram, ("lat", "lon"))
    lower = jnp.linalg.cholesky(gram)
    upper = lower.T
    cells = field.shape[1] * width_lon * width_lat * lax.axis_size("lat") * lax.axis_size("lon")
    scale = jnp.sqrt(jnp.float32(cells))
    result = basis(lower_inverse(lower), scale.reshape(1, 1), field)
    return (result, upper / scale)


def solution(mesh):
    placed = (
        P(None, None, "lon", "lat"),
        P(None, None, "lon", "lat"),
        P(None, None, "lon", "lat"),
        P(None, "lon", "lat"),
    )
    return jax.shard_map(
        body,
        mesh=mesh,
        in_specs=placed,
        out_specs=(P(None, None, "lon", "lat"), P()),
        check_vma=False,
    )
```

```python
import jax
import jax.numpy as jnp
from jax import lax
from jax.experimental import pallas as pl
from jax.experimental.pallas import tpu as pltpu
from jax.sharding import PartitionSpec as P

STEPS = 4
HALO = 2 * STEPS
GROUP = 8

diffuse = 0.24


def lower_inverse(lower):
    eye = jnp.eye(lower.shape[0], dtype=lower.dtype)
    return lax.linalg.triangular_solve(lower, eye, left_side=True, lower=True)


def all_sum(value, axes):
    for axis in axes:
        count = lax.axis_size(axis)
        if count & (count - 1):
            value = lax.psum(value, axis)
            continue
        stride = 1
        while stride < count:
            value = value + lax.ppermute(value, axis, [(i, i ^ stride) for i in range(count)])
            stride *= 2
    return value


def shifted(x, offset, axis):
    n = x.shape[axis]
    return pltpu.roll(x, (-offset) % n, axis)


def transport_kernel(
    mask_ref, pr_ref, wi_ref, te_ref, ob_ref, ln_ref, lp_ref, un_ref, up_ref, o_ref, g_ref, coef_ref, plane_ref
):
    k = diffuse
    c0 = 1.0 - 4.0 * diffuse
    probes = o_ref.shape[0]
    rows = o_ref.shape[2]
    lanes = o_ref.shape[3]
    full_rows, full_lanes = plane_ref.shape[1:]
    mask = mask_ref[...]

    def masked(f):
        return (f.reshape(full_rows // 8, 8, full_lanes) * mask[None]).reshape(full_rows, full_lanes)

    def assemble(own, plane, slot=0):
        plane_ref[slot, 0:rows, 0:lanes] = own
        plane_ref[slot, rows : rows + HALO, 0:lanes] = ln_ref[0, plane]
        plane_ref[slot, rows + HALO : full_rows, 0:lanes] = lp_ref[0, plane]
        gap = jnp.zeros((lanes - 2 * HALO, lanes), jnp.float32)
        halo = jnp.concatenate((un_ref[0, plane], gap, up_ref[0, plane]), axis=0)
        plane_ref[slot, :, lanes:full_lanes] = halo.T[:full_rows]
        return plane_ref[slot]

    w_east = assemble(wi_ref[0, 0], probes + 0)
    w_north = assemble(wi_ref[1, 0], probes + 1)
    t_east = assemble(te_ref[0, 0], probes + 2)
    t_north = assemble(te_ref[1, 0], probes + 3)
    for s in range(STEPS):
        east = 0.5 * (w_east + s * t_east)
        north = 0.5 * (w_north + s * t_north)
        coef_ref[s, 0] = k - east
        coef_ref[s, 1] = k + east
        coef_ref[s, 2] = k - north
        coef_ref[s, 3] = k + north
        coef_ref[s, 4] = shifted(k - east, -1, 0)
        coef_ref[s, 5] = shifted(k + east, 1, 0)
        coef_ref[s, 6] = shifted(k - north, -1, 1)
        coef_ref[s, 7] = shifted(k + north, 1, 1)
    coef_ref[STEPS, 0] = assemble(ob_ref[0], probes + 4)

    def probe_pair(i, carry):
        p = GROUP * i
        fs = [assemble(pr_ref[p + j, 0], p + j, j) for j in range(GROUP)]
        for s in range(STEPS):
            ce_m, ce_p, cn_m, cn_p = (coef_ref[s, c] for c in range(4))
            fs = [
                masked(
                    c0 * f
                    + ce_m * shifted(f, 1, 0)
                    + ce_p * shifted(f, -1, 0)
                    + cn_m * shifted(f, 1, 1)
                    + cn_p * shifted(f, -1, 1)
                )
                for f in fs
            ]
        weight = coef_ref[STEPS, 0]
        fs = [f * weight for f in fs]
        for s in reversed(range(STEPS)):
            aw, ae, as_, an = (coef_ref[s, c] for c in range(4, 8))
            fs = [
                masked(
                    c0 * f
                    + aw * shifted(f, -1, 0)
                    + ae * shifted(f, 1, 0)
                    + as_ * shifted(f, -1, 1)
                    + an * shifted(f, 1, 1)
                )
                for f in fs
            ]
        for j in range(GROUP):
            o_ref[p + j, 0] = fs[j][:rows, :lanes]
        return carry

    lax.fori_loop(0, probes // GROUP, probe_pair, 0)
    for p in range(probes):
        for q in range(p, probes):
            prod = (o_ref[p, 0] * o_ref[q, 0]).reshape(rows // 8, 8, lanes)
            part = jnp.sum(jnp.sum(prod, axis=0), axis=0, keepdims=True)
            g_ref[0, pl.ds(p * probes + q, 1), :] = part
            if q != p:
                g_ref[0, pl.ds(q * probes + p, 1), :] = part


def transport(mask, probes, wind, wind_tend, obs_weight, lon_next, lon_prev, lat_next, lat_prev):
    n_probes, levels, rows, lanes = probes.shape
    planes = lon_next.shape[1]
    full_rows = rows + 2 * HALO
    full_lanes = 2 * lanes

    def level_block(lead):
        return pl.BlockSpec((lead, 1, rows, lanes), lambda l: (0, l, 0, 0))

    def halo_block(height):
        return pl.BlockSpec((1, planes, height, lanes), lambda l: (l, 0, 0, 0))

    return pl.pallas_call(
        transport_kernel,
        grid=(levels,),
        in_specs=[
            pl.BlockSpec((8, full_lanes), lambda l: (0, 0)),
            level_block(n_probes),
            level_block(2),
            level_block(2),
            pl.BlockSpec((1, rows, lanes), lambda l: (l, 0, 0)),
            halo_block(HALO),
            halo_block(HALO),
            halo_block(HALO),
            halo_block(HALO),
        ],
        out_specs=[
            level_block(n_probes),
            pl.BlockSpec((1, n_probes * n_probes, lanes), lambda l: (l, 0, 0)),
        ],
        out_shape=[
            jax.ShapeDtypeStruct((n_probes, levels, rows, lanes), jnp.float32),
            jax.ShapeDtypeStruct((levels, n_probes * n_probes, lanes), jnp.float32),
        ],
        scratch_shapes=[
            pltpu.VMEM((STEPS + 1, 8, full_rows, full_lanes), jnp.float32),
            pltpu.VMEM((GROUP, full_rows, full_lanes), jnp.float32),
        ],
    )(mask, probes, wind, wind_tend, obs_weight, lon_next, lon_prev, lat_next, lat_prev)

def basis_kernel(inv_ref, scale_ref, z_ref, o_ref):
    probes, levels, rows = z_ref.shape[:3]
    scale = scale_ref[0, 0]
    chunks = rows // 8

    def chunk(c, carry):
        level = c // chunks
        part = pl.ds((c % chunks) * 8, 8)
        z = [z_ref[q, level, part, :] for q in range(probes)]
        for p in range(probes):
            acc = inv_ref[p, 0] * z[0]
            for q in range(1, probes):
                acc = acc + inv_ref[p, q] * z[q]
            o_ref[p, level, part, :] = acc * scale
        return carry

    lax.fori_loop(0, levels * chunks, chunk, 0)


def basis(inverse, scale, field):
    whole = pl.BlockSpec(field.shape, lambda i: (0, 0, 0, 0))
    return pl.pallas_call(
        basis_kernel,
        grid=(1,),
        in_specs=[
            pl.BlockSpec(memory_space=pltpu.SMEM),
            pl.BlockSpec(memory_space=pltpu.SMEM),
            whole,
        ],
        out_specs=whole,
        out_shape=jax.ShapeDtypeStruct(field.shape, jnp.float32),
    )(inverse, scale, field)

def body(probes, wind, wind_tend, obs_weight):
    n_probes, levels, width_lon, width_lat = probes.shape

    def planes_of(part):
        return jnp.concatenate(
            (
                jnp.swapaxes(part(probes), 0, 1),
                jnp.swapaxes(part(wind), 0, 1),
                jnp.swapaxes(part(wind_tend), 0, 1),
                part(obs_weight[None])[0][:, None],
            ),
            axis=1,
        )

    heads = planes_of(lambda a: a[..., :HALO, :])
    tails = planes_of(lambda a: a[..., width_lon - HALO :, :])
    n_lon = lax.axis_size("lon")
    lon_next = lax.ppermute(heads, "lon", [((i + 1) % n_lon, i) for i in range(n_lon)])
    lon_prev = lax.ppermute(tails, "lon", [(i, (i + 1) % n_lon) for i in range(n_lon)])
    own_lo = planes_of(lambda a: a[..., :HALO])
    own_hi = planes_of(lambda a: a[..., width_lat - HALO :])
    fill = jnp.zeros(own_lo.shape[:2] + (width_lat - width_lon - 2 * HALO, HALO), jnp.float32)
    edge_lo = jnp.concatenate((own_lo, lon_next[..., :HALO], lon_prev[..., :HALO], fill), axis=2)
    edge_hi = jnp.concatenate(
        (own_hi, lon_next[..., width_lat - HALO :], lon_prev[..., width_lat - HALO :], fill), axis=2
    )
    n_lat = lax.axis_size("lat")
    lat_next = lax.ppermute(jnp.swapaxes(edge_lo, 2, 3), "lat", [(j + 1, j) for j in range(n_lat - 1)])
    lat_prev = lax.ppermute(jnp.swapaxes(edge_hi, 2, 3), "lat", [(j, j + 1) for j in range(n_lat - 1)])
    lanes = 2 * width_lat
    lane = lax.broadcasted_iota(jnp.int32, (8, lanes), 1)
    start = lax.axis_index("lat") * width_lat
    cell = jnp.where(lane < width_lat + HALO, start + lane, start + lane - lanes)
    inside = ((lane < width_lat + HALO) | (lane >= lanes - HALO)) & (cell >= 0)
    inside = inside & (cell < width_lat * n_lat)
    mask = inside.astype(jnp.float32)

    field, partial = transport(
        mask, probes, wind, wind_tend, obs_weight, lon_next, lon_prev, lat_next, lat_prev
    )

    gram = jnp.sum(partial, axis=(0, 2)).reshape(n_probes, n_probes)
    gram = all_sum(gram, ("lon", "lat"))
    lower = jnp.linalg.cholesky(gram)
    upper = lower.T
    cells = field.shape[1] * width_lon * width_lat * lax.axis_size("lat") * lax.axis_size("lon")
    scale = jnp.sqrt(jnp.float32(cells))
    result = basis(lower_inverse(lower), scale.reshape(1, 1), field)
    return (result, upper / scale)


def solution(mesh):
    placed = (
        P(None, None, "lon", "lat"),
        P(None, None, "lon", "lat"),
        P(None, None, "lon", "lat"),
        P(None, "lon", "lat"),
    )
    return jax.shard_map(
        body,
        mesh=mesh,
        in_specs=placed,
        out_specs=(P(None, None, "lon", "lat"), P()),
        check_vma=False,
    )
```

```python
import jax
import jax.numpy as jnp
from jax import lax
from jax.experimental import pallas as pl
from jax.experimental.pallas import tpu as pltpu
from jax.sharding import PartitionSpec as P

STEPS = 4
HALO = 2 * STEPS
GROUP = 8

diffuse = 0.24


def lower_inverse(lower):
    eye = jnp.eye(lower.shape[0], dtype=lower.dtype)
    return lax.linalg.triangular_solve(lower, eye, left_side=True, lower=True)


def all_sum(value, axes):
    for axis in axes:
        count = lax.axis_size(axis)
        if count & (count - 1):
            value = lax.psum(value, axis)
            continue
        stride = 1
        while stride < count:
            value = value + lax.ppermute(value, axis, [(i, i ^ stride) for i in range(count)])
            stride *= 2
    return value


def shifted(x, offset, axis):
    n = x.shape[axis]
    return pltpu.roll(x, (-offset) % n, axis)


def transport_kernel(
    mask_ref, pr_ref, wi_ref, te_ref, ob_ref, ln_ref, lp_ref, un_ref, up_ref, o_ref, g_ref, coef_ref, plane_ref
):
    k = diffuse
    c0 = 1.0 - 4.0 * diffuse
    probes = o_ref.shape[0]
    rows = o_ref.shape[2]
    lanes = o_ref.shape[3]
    full_rows, full_lanes = plane_ref.shape[1:]
    mask = mask_ref[...]

    def masked(f):
        return (f.reshape(full_rows // 8, 8, full_lanes) * mask[None]).reshape(full_rows, full_lanes)

    def assemble(own, plane, slot=0):
        plane_ref[slot, 0:rows, 0:lanes] = own
        plane_ref[slot, rows : rows + HALO, 0:lanes] = ln_ref[0, plane]
        plane_ref[slot, rows + HALO : full_rows, 0:lanes] = lp_ref[0, plane]
        gap = jnp.zeros((lanes - 2 * HALO, lanes), jnp.float32)
        halo = jnp.concatenate((un_ref[0, plane], gap, up_ref[0, plane]), axis=0)
        plane_ref[slot, :, lanes:full_lanes] = halo.T[:full_rows]
        return plane_ref[slot]

    w_east = assemble(wi_ref[0, 0], probes + 0)
    w_north = assemble(wi_ref[1, 0], probes + 1)
    t_east = assemble(te_ref[0, 0], probes + 2)
    t_north = assemble(te_ref[1, 0], probes + 3)
    for s in range(STEPS):
        east = 0.5 * (w_east + s * t_east)
        north = 0.5 * (w_north + s * t_north)
        coef_ref[s, 0] = k - east
        coef_ref[s, 1] = k + east
        coef_ref[s, 2] = k - north
        coef_ref[s, 3] = k + north
        coef_ref[s, 4] = shifted(k - east, -1, 0)
        coef_ref[s, 5] = shifted(k + east, 1, 0)
        coef_ref[s, 6] = shifted(k - north, -1, 1)
        coef_ref[s, 7] = shifted(k + north, 1, 1)
    coef_ref[STEPS, 0] = assemble(ob_ref[0], probes + 4)

    def probe_pair(i, carry):
        p = GROUP * i
        fs = [assemble(pr_ref[p + j, 0], p + j, j) for j in range(GROUP)]
        for s in range(STEPS):
            ce_m, ce_p, cn_m, cn_p = (coef_ref[s, c] for c in range(4))
            fs = [
                masked(
                    c0 * f
                    + ce_m * shifted(f, 1, 0)
                    + ce_p * shifted(f, -1, 0)
                    + cn_m * shifted(f, 1, 1)
                    + cn_p * shifted(f, -1, 1)
                )
                for f in fs
            ]
        weight = coef_ref[STEPS, 0]
        fs = [f * weight for f in fs]
        for s in reversed(range(STEPS)):
            aw, ae, as_, an = (coef_ref[s, c] for c in range(4, 8))
            fs = [
                masked(
                    c0 * f
                    + aw * shifted(f, -1, 0)
                    + ae * shifted(f, 1, 0)
                    + as_ * shifted(f, -1, 1)
                    + an * shifted(f, 1, 1)
                )
                for f in fs
            ]
        for j in range(GROUP):
            o_ref[p + j, 0] = fs[j][:rows, :lanes]
        return carry

    lax.fori_loop(0, probes // GROUP, probe_pair, 0)
    @pl.when(pl.program_id(0) == 0)
    def _():
        g_ref[...] = jnp.zeros(g_ref.shape, jnp.float32)

    for p in range(probes):
        for q in range(p, probes):
            prod = (o_ref[p, 0] * o_ref[q, 0]).reshape(rows // 8, 8, lanes)
            part = jnp.sum(jnp.sum(prod, axis=0), axis=0, keepdims=True)
            g_ref[pl.ds(p * probes + q, 1), :] += part
            if q != p:
                g_ref[pl.ds(q * probes + p, 1), :] += part


def transport(mask, probes, wind, wind_tend, obs_weight, lon_next, lon_prev, lat_next, lat_prev):
    n_probes, levels, rows, lanes = probes.shape
    planes = lon_next.shape[1]
    full_rows = rows + 2 * HALO
    full_lanes = 2 * lanes

    def level_block(lead):
        return pl.BlockSpec((lead, 1, rows, lanes), lambda l: (0, l, 0, 0))

    def halo_block(height):
        return pl.BlockSpec((1, planes, height, lanes), lambda l: (l, 0, 0, 0))

    return pl.pallas_call(
        transport_kernel,
        grid=(levels,),
        in_specs=[
            pl.BlockSpec((8, full_lanes), lambda l: (0, 0)),
            level_block(n_probes),
            level_block(2),
            level_block(2),
            pl.BlockSpec((1, rows, lanes), lambda l: (l, 0, 0)),
            halo_block(HALO),
            halo_block(HALO),
            halo_block(HALO),
            halo_block(HALO),
        ],
        out_specs=[
            level_block(n_probes),
            pl.BlockSpec((n_probes * n_probes, lanes), lambda l: (0, 0)),
        ],
        out_shape=[
            jax.ShapeDtypeStruct((n_probes, levels, rows, lanes), jnp.float32),
            jax.ShapeDtypeStruct((n_probes * n_probes, lanes), jnp.float32),
        ],
        scratch_shapes=[
            pltpu.VMEM((STEPS + 1, 8, full_rows, full_lanes), jnp.float32),
            pltpu.VMEM((GROUP, full_rows, full_lanes), jnp.float32),
        ],
    )(mask, probes, wind, wind_tend, obs_weight, lon_next, lon_prev, lat_next, lat_prev)

def basis_kernel(inv_ref, scale_ref, z_ref, o_ref):
    probes, levels, rows = z_ref.shape[:3]
    scale = scale_ref[0, 0]
    chunks = rows // 8

    def chunk(c, carry):
        level = c // chunks
        part = pl.ds((c % chunks) * 8, 8)
        z = [z_ref[q, level, part, :] for q in range(probes)]
        for p in range(probes):
            acc = inv_ref[p, 0] * z[0]
            for q in range(1, probes):
                acc = acc + inv_ref[p, q] * z[q]
            o_ref[p, level, part, :] = acc * scale
        return carry

    lax.fori_loop(0, levels * chunks, chunk, 0)


def basis(inverse, scale, field):
    whole = pl.BlockSpec(field.shape, lambda i: (0, 0, 0, 0))
    return pl.pallas_call(
        basis_kernel,
        grid=(1,),
        in_specs=[
            pl.BlockSpec(memory_space=pltpu.SMEM),
            pl.BlockSpec(memory_space=pltpu.SMEM),
            whole,
        ],
        out_specs=whole,
        out_shape=jax.ShapeDtypeStruct(field.shape, jnp.float32),
    )(inverse, scale, field)

def body(probes, wind, wind_tend, obs_weight):
    n_probes, levels, width_lon, width_lat = probes.shape

    def planes_of(part):
        return jnp.concatenate(
            (
                jnp.swapaxes(part(probes), 0, 1),
                jnp.swapaxes(part(wind), 0, 1),
                jnp.swapaxes(part(wind_tend), 0, 1),
                part(obs_weight[None])[0][:, None],
            ),
            axis=1,
        )

    heads = planes_of(lambda a: a[..., :HALO, :])
    tails = planes_of(lambda a: a[..., width_lon - HALO :, :])
    n_lon = lax.axis_size("lon")
    lon_next = lax.ppermute(heads, "lon", [((i + 1) % n_lon, i) for i in range(n_lon)])
    lon_prev = lax.ppermute(tails, "lon", [(i, (i + 1) % n_lon) for i in range(n_lon)])
    own_lo = planes_of(lambda a: a[..., :HALO])
    own_hi = planes_of(lambda a: a[..., width_lat - HALO :])
    fill = jnp.zeros(own_lo.shape[:2] + (width_lat - width_lon - 2 * HALO, HALO), jnp.float32)
    edge_lo = jnp.concatenate((own_lo, lon_next[..., :HALO], lon_prev[..., :HALO], fill), axis=2)
    edge_hi = jnp.concatenate(
        (own_hi, lon_next[..., width_lat - HALO :], lon_prev[..., width_lat - HALO :], fill), axis=2
    )
    n_lat = lax.axis_size("lat")
    lat_next = lax.ppermute(jnp.swapaxes(edge_lo, 2, 3), "lat", [(j + 1, j) for j in range(n_lat - 1)])
    lat_prev = lax.ppermute(jnp.swapaxes(edge_hi, 2, 3), "lat", [(j, j + 1) for j in range(n_lat - 1)])
    lanes = 2 * width_lat
    lane = lax.broadcasted_iota(jnp.int32, (8, lanes), 1)
    start = lax.axis_index("lat") * width_lat
    cell = jnp.where(lane < width_lat + HALO, start + lane, start + lane - lanes)
    inside = ((lane < width_lat + HALO) | (lane >= lanes - HALO)) & (cell >= 0)
    inside = inside & (cell < width_lat * n_lat)
    mask = inside.astype(jnp.float32)

    field, partial = transport(
        mask, probes, wind, wind_tend, obs_weight, lon_next, lon_prev, lat_next, lat_prev
    )

    gram = jnp.sum(partial, axis=1).reshape(n_probes, n_probes)
    gram = all_sum(gram, ("lon", "lat"))
    lower = jnp.linalg.cholesky(gram)
    upper = lower.T
    cells = field.shape[1] * width_lon * width_lat * lax.axis_size("lat") * lax.axis_size("lon")
    scale = jnp.sqrt(jnp.float32(cells))
    result = basis(lower_inverse(lower), scale.reshape(1, 1), field)
    return (result, upper / scale)


def solution(mesh):
    placed = (
        P(None, None, "lon", "lat"),
        P(None, None, "lon", "lat"),
        P(None, None, "lon", "lat"),
        P(None, "lon", "lat"),
    )
    return jax.shard_map(
        body,
        mesh=mesh,
        in_specs=placed,
        out_specs=(P(None, None, "lon", "lat"), P()),
        check_vma=False,
    )
```

```python
import functools

import numpy as np
import jax
import jax.numpy as jnp
from jax import lax
from jax.experimental import pallas as pl
from jax.experimental.pallas import tpu as pltpu
from jax.sharding import PartitionSpec as P

STEPS = 4
HALO = 2 * STEPS
GROUP = 8

diffuse = 0.24


def lower_inverse(lower):
    eye = jnp.eye(lower.shape[0], dtype=lower.dtype)
    return lax.linalg.triangular_solve(lower, eye, left_side=True, lower=True)


def all_sum(value, axes):
    for axis in axes:
        count = lax.axis_size(axis)
        if count & (count - 1):
            value = lax.psum(value, axis)
            continue
        stride = 1
        while stride < count:
            value = value + lax.ppermute(value, axis, [(i, i ^ stride) for i in range(count)])
            stride *= 2
    return value


def shifted(x, offset, axis):
    n = x.shape[axis]
    return pltpu.roll(x, (-offset) % n, axis)


def transport_kernel(
    mask_ref, pr_ref, wi_ref, te_ref, ob_ref, ln_ref, lp_ref, un_ref, up_ref, o_ref, g_ref, coef_ref, plane_ref
):
    k = diffuse
    c0 = 1.0 - 4.0 * diffuse
    probes = o_ref.shape[0]
    rows = o_ref.shape[2]
    lanes = o_ref.shape[3]
    full_rows, full_lanes = plane_ref.shape[1:]
    mask = mask_ref[...]

    def masked(f):
        return (f.reshape(full_rows // 8, 8, full_lanes) * mask[None]).reshape(full_rows, full_lanes)

    def assemble(own, plane, slot=0):
        plane_ref[slot, 0:rows, 0:lanes] = own
        plane_ref[slot, rows : rows + HALO, 0:lanes] = ln_ref[0, plane]
        plane_ref[slot, rows + HALO : full_rows, 0:lanes] = lp_ref[0, plane]
        gap = jnp.zeros((lanes - 2 * HALO, lanes), jnp.float32)
        halo = jnp.concatenate((un_ref[0, plane], gap, up_ref[0, plane]), axis=0)
        plane_ref[slot, :, lanes:full_lanes] = halo.T[:full_rows]
        return plane_ref[slot]

    w_east = assemble(wi_ref[0, 0], probes + 0)
    w_north = assemble(wi_ref[1, 0], probes + 1)
    t_east = assemble(te_ref[0, 0], probes + 2)
    t_north = assemble(te_ref[1, 0], probes + 3)
    for s in range(STEPS):
        east = 0.5 * (w_east + s * t_east)
        north = 0.5 * (w_north + s * t_north)
        coef_ref[s, 0] = k - east
        coef_ref[s, 1] = k + east
        coef_ref[s, 2] = k - north
        coef_ref[s, 3] = k + north
        coef_ref[s, 4] = shifted(k - east, -1, 0)
        coef_ref[s, 5] = shifted(k + east, 1, 0)
        coef_ref[s, 6] = shifted(k - north, -1, 1)
        coef_ref[s, 7] = shifted(k + north, 1, 1)
    coef_ref[STEPS, 0] = assemble(ob_ref[0], probes + 4)

    def probe_pair(i, carry):
        p = GROUP * i
        fs = [assemble(pr_ref[p + j, 0], p + j, j) for j in range(GROUP)]
        for s in range(STEPS):
            ce_m, ce_p, cn_m, cn_p = (coef_ref[s, c] for c in range(4))
            fs = [
                masked(
                    c0 * f
                    + ce_m * shifted(f, 1, 0)
                    + ce_p * shifted(f, -1, 0)
                    + cn_m * shifted(f, 1, 1)
                    + cn_p * shifted(f, -1, 1)
                )
                for f in fs
            ]
        weight = coef_ref[STEPS, 0]
        fs = [f * weight for f in fs]
        for s in reversed(range(STEPS)):
            aw, ae, as_, an = (coef_ref[s, c] for c in range(4, 8))
            fs = [
                masked(
                    c0 * f
                    + aw * shifted(f, -1, 0)
                    + ae * shifted(f, 1, 0)
                    + as_ * shifted(f, -1, 1)
                    + an * shifted(f, 1, 1)
                )
                for f in fs
            ]
        for j in range(GROUP):
            o_ref[p + j, 0] = fs[j][:rows, :lanes]
        return carry

    lax.fori_loop(0, probes // GROUP, probe_pair, 0)
    for p in range(probes):
        for q in range(p, probes):
            prod = (o_ref[p, 0] * o_ref[q, 0]).reshape(rows // 8, 8, lanes)
            part = jnp.sum(jnp.sum(prod, axis=0), axis=0, keepdims=True)
            g_ref[0, pl.ds(p * probes + q, 1), :] = part
            if q != p:
                g_ref[0, pl.ds(q * probes + p, 1), :] = part


def transport(mask, probes, wind, wind_tend, obs_weight, lon_next, lon_prev, lat_next, lat_prev):
    n_probes, levels, rows, lanes = probes.shape
    planes = lon_next.shape[1]
    full_rows = rows + 2 * HALO
    full_lanes = 2 * lanes

    def level_block(lead):
        return pl.BlockSpec((lead, 1, rows, lanes), lambda l: (0, l, 0, 0))

    def halo_block(height):
        return pl.BlockSpec((1, planes, height, lanes), lambda l: (l, 0, 0, 0))

    return pl.pallas_call(
        transport_kernel,
        grid=(levels,),
        in_specs=[
            pl.BlockSpec((8, full_lanes), lambda l: (0, 0)),
            level_block(n_probes),
            level_block(2),
            level_block(2),
            pl.BlockSpec((1, rows, lanes), lambda l: (l, 0, 0)),
            halo_block(HALO),
            halo_block(HALO),
            halo_block(HALO),
            halo_block(HALO),
        ],
        out_specs=[
            level_block(n_probes),
            pl.BlockSpec((1, n_probes * n_probes, lanes), lambda l: (l, 0, 0)),
        ],
        out_shape=[
            jax.ShapeDtypeStruct((n_probes, levels, rows, lanes), jnp.float32),
            jax.ShapeDtypeStruct((levels, n_probes * n_probes, lanes), jnp.float32),
        ],
        scratch_shapes=[
            pltpu.VMEM((STEPS + 1, 8, full_rows, full_lanes), jnp.float32),
            pltpu.VMEM((GROUP, full_rows, full_lanes), jnp.float32),
        ],
    )(mask, probes, wind, wind_tend, obs_weight, lon_next, lon_prev, lat_next, lat_prev)

def basis_kernel(inv_ref, z_ref, o_ref, *, scale):
    probes, levels, rows = z_ref.shape[:3]
    chunks = rows // 8

    def chunk(c, carry):
        level = c // chunks
        part = pl.ds((c % chunks) * 8, 8)
        z = [z_ref[q, level, part, :] for q in range(probes)]
        for p in range(probes):
            acc = inv_ref[p, 0] * z[0]
            for q in range(1, probes):
                acc = acc + inv_ref[p, q] * z[q]
            o_ref[p, level, part, :] = acc * scale
        return carry

    lax.fori_loop(0, levels * chunks, chunk, 0)


def basis(inverse, scale, field):
    whole = pl.BlockSpec(field.shape, lambda i: (0, 0, 0, 0))
    return pl.pallas_call(
        functools.partial(basis_kernel, scale=scale),
        grid=(1,),
        in_specs=[
            pl.BlockSpec(memory_space=pltpu.SMEM),
            whole,
        ],
        out_specs=whole,
        out_shape=jax.ShapeDtypeStruct(field.shape, jnp.float32),
    )(inverse, field)

def body(probes, wind, wind_tend, obs_weight):
    n_probes, levels, width_lon, width_lat = probes.shape

    def planes_of(part):
        return jnp.concatenate(
            (
                jnp.swapaxes(part(probes), 0, 1),
                jnp.swapaxes(part(wind), 0, 1),
                jnp.swapaxes(part(wind_tend), 0, 1),
                part(obs_weight[None])[0][:, None],
            ),
            axis=1,
        )

    heads = planes_of(lambda a: a[..., :HALO, :])
    tails = planes_of(lambda a: a[..., width_lon - HALO :, :])
    n_lon = lax.axis_size("lon")
    lon_next = lax.ppermute(heads, "lon", [((i + 1) % n_lon, i) for i in range(n_lon)])
    lon_prev = lax.ppermute(tails, "lon", [(i, (i + 1) % n_lon) for i in range(n_lon)])
    own_lo = planes_of(lambda a: a[..., :HALO])
    own_hi = planes_of(lambda a: a[..., width_lat - HALO :])
    fill = jnp.zeros(own_lo.shape[:2] + (width_lat - width_lon - 2 * HALO, HALO), jnp.float32)
    edge_lo = jnp.concatenate((own_lo, lon_next[..., :HALO], lon_prev[..., :HALO], fill), axis=2)
    edge_hi = jnp.concatenate(
        (own_hi, lon_next[..., width_lat - HALO :], lon_prev[..., width_lat - HALO :], fill), axis=2
    )
    n_lat = lax.axis_size("lat")
    lat_next = lax.ppermute(jnp.swapaxes(edge_lo, 2, 3), "lat", [(j + 1, j) for j in range(n_lat - 1)])
    lat_prev = lax.ppermute(jnp.swapaxes(edge_hi, 2, 3), "lat", [(j, j + 1) for j in range(n_lat - 1)])
    lanes = 2 * width_lat
    lane = lax.broadcasted_iota(jnp.int32, (8, lanes), 1)
    start = lax.axis_index("lat") * width_lat
    cell = jnp.where(lane < width_lat + HALO, start + lane, start + lane - lanes)
    inside = ((lane < width_lat + HALO) | (lane >= lanes - HALO)) & (cell >= 0)
    inside = inside & (cell < width_lat * n_lat)
    mask = inside.astype(jnp.float32)

    field, partial = transport(
        mask, probes, wind, wind_tend, obs_weight, lon_next, lon_prev, lat_next, lat_prev
    )

    gram = jnp.sum(partial, axis=(0, 2)).reshape(n_probes, n_probes)
    gram = all_sum(gram, ("lon", "lat"))
    lower = jnp.linalg.cholesky(gram)
    upper = lower.T
    cells = field.shape[1] * width_lon * width_lat * lax.axis_size("lat") * lax.axis_size("lon")
    scale = jnp.sqrt(jnp.float32(cells))
    result = basis(lower_inverse(lower), float(np.sqrt(np.float32(cells))), field)
    return (result, upper / scale)


def solution(mesh):
    placed = (
        P(None, None, "lon", "lat"),
        P(None, None, "lon", "lat"),
        P(None, None, "lon", "lat"),
        P(None, "lon", "lat"),
    )
    return jax.shard_map(
        body,
        mesh=mesh,
        in_specs=placed,
        out_specs=(P(None, None, "lon", "lat"), P()),
        check_vma=False,
    )
```
